128 devices in a mesh: dev: 128 (over y, z, x, core).
Axes of the slice: x: 4, y: 4, z: 4, core: 2. Of those that a mesh axis runs over, the one named last changes fastest.
Arguments:
- records: bfloat16 [8192, 2048], P('dev'), may hold values from -100 to 100
- record_station: int32 [8192], P('dev'), may hold values from 0 to 8191, as said below
- taps: bfloat16 [8192, 255], P('dev'), may hold values from -0.375 to 0.375
- gap_mask: int32 [8192, 4], P('dev'), may hold values 0 or 1
- partners: int32 [3, 128], replicated, may hold values from 0 to 127, as said below
Outputs:
- correlations: bfloat16 [3, 8192, 64, 512], P(None, 'dev')
The draws below stay inside these ranges and needn't reach their ends.
Inputs may be any that keep to these rules, and one draw needn't show every extreme that they name: `record_station`: every station appears exactly once; the 64 records of one device belong to 64 different station blocks, exactly one record to each; among them is one record of the block half the axis away from the device, (d + 64) mod 128 for device d. `partners`: in round r block b is paired with block b XOR c_r, for a code c_r of 1 to 127 that differs from round to round.
All inputs are finite; a program needn't handle non-finite values. No bound on the sum of `gap_mask` on one device may be relied on, other than what follows from the above.
Results may differ from the reference program's by a relative error of at most 0.0092.
Values may be sent and summed in bfloat16 or wider, within the bound.
No kernel may reach another device: no remote copies, remote signals or barrier semaphores. Data moves between devices by JAX's collectives and lax.ppermute only.
A program may use at most 128 MiB of HBM per device.

```python
import math
import jax
import jax.numpy as jnp
from jax import lax

SEG = 512
TAPS = 255
SPB = 64
NSEG = 4
ROUNDS = 3
BLOCKS = 128
CAP = 1
STATIONS = 8192
NSAMP = 2048


def draw_records(key, part):
    scale_key, noise_key = jax.random.split(key, 2)
    scales = jnp.exp(jax.random.uniform(scale_key, (STATIONS, NSEG, 1), jnp.float32, 0.0, math.log(10.0)))
    values = scales * jax.random.truncated_normal(noise_key, -4.0, 4.0, (STATIONS, NSEG, SEG), jnp.float32)
    return values.reshape(STATIONS, NSAMP).astype(jnp.bfloat16)


def draw_record_station(key, part):
    offset_key, order_key = jax.random.split(key, 2)
    groups = SPB // CAP
    half = BLOCKS // 2
    drawn = jax.random.permutation(offset_key, BLOCKS - 1).astype(jnp.int32)
    others = jnp.where(drawn >= half, drawn + 1, drawn).astype(jnp.int32)
    offsets = jnp.concatenate([jnp.full((1,), half, jnp.int32), others[:groups - 1]]).astype(jnp.int32)
    sources = jnp.arange(BLOCKS, dtype=jnp.int32)[:, None]
    places = jnp.arange(SPB, dtype=jnp.int32)[None, :]
    group_of = places // CAP
    owners = (sources - offsets[group_of] + BLOCKS) % BLOCKS
    stations = owners * SPB + group_of * CAP + places % CAP
    row_keys = jax.random.split(order_key, BLOCKS)
    orders = jax.vmap(lambda row_key: jax.random.permutation(row_key, SPB))(row_keys).astype(jnp.int32)
    shuffled = jnp.take_along_axis(stations, orders, axis=1)
    return shuffled.reshape(STATIONS).astype(jnp.int32)


def draw_partners(key, part):
    codes = jax.random.permutation(key, BLOCKS - 1)[:ROUNDS].astype(jnp.int32) + 1
    numbers = jnp.arange(BLOCKS, dtype=jnp.int32)
    return jnp.bitwise_xor(numbers[None, :], codes[:, None]).astype(jnp.int32)


def plant(result, stream_key, least, high):
    longest = result.shape.index(max(result.shape))
    spots = []
    for shift in (0, 1):
        where = [jax.random.randint(jax.random.fold_in(stream_key, axis), (), 0, length) for axis, length in enumerate(result.shape)]
        where[longest] = (where[longest] + shift) % result.shape[longest]
        spots.append(tuple(where))
    return result.at[spots[0]].set(least).at[spots[1]].set(high)


def level_of(own_key, extent, cuts, least, largest):
    def one(dim, blocks):
        steps = jax.random.uniform(jax.random.fold_in(jax.random.fold_in(own_key, 6), dim), (blocks,), jnp.float32, least / len(cuts), largest / len(cuts))
        return jnp.repeat(jnp.exp(steps), extent[dim] // blocks).reshape((-1,) + (1,) * (len(extent) - dim - 1))

    level = one(*cuts[0])
    for cut in cuts[1:]:
        level = level * one(*cut)
    return level


def scatter_about(own_key, extent, spread, limit, cuts=(), kind=jnp.bfloat16):
    values = spread * jax.random.normal(own_key, extent, jnp.float32)
    if cuts:
        values = values * level_of(own_key, extent, cuts, -0.22, 0.18)
    return jnp.clip(values, -limit, limit).astype(kind)


def setup_inputs(seed: int = 0) -> dict:
    arg_keys = jax.random.split(jax.random.key(seed), 6)
    records = draw_records(jax.random.fold_in(arg_keys[5], 71), 0)
    record_station = draw_record_station(jax.random.fold_in(arg_keys[5], 71), 0)
    taps = scatter_about(arg_keys[2], (STATIONS, TAPS), TAPS ** -0.5, 0.375, ((0, 128),))
    gap_mask = plant((jax.random.randint(arg_keys[3], (STATIONS, NSEG), 0, 5) < 3).astype(jnp.int32), jax.random.fold_in(arg_keys[3], 1), 0, 1)
    partners = draw_partners(jax.random.fold_in(arg_keys[5], 71), 0)
    return {"records": records, "record_station": record_station, "taps": taps, "gap_mask": gap_mask, "partners": partners}


def angle_table(row_count, col_count):
    first = jnp.arange(row_count, dtype=jnp.int32)[:, None]
    second = jnp.arange(col_count, dtype=jnp.int32)[None, :]
    return 2.0 * math.pi / SEG * (first * second % SEG).astype(jnp.float32)

def forward_table(row_count):
    phase = angle_table(row_count, SEG // 2)
    return jnp.concatenate([jnp.cos(phase), -jnp.sin(phase)], axis=1).astype(jnp.bfloat16)

def inverse_table():
    phase = angle_table(SEG // 2, SEG)
    weights = jnp.where(jnp.arange(SEG // 2, dtype=jnp.int32) == 0, 1.0, 2.0).astype(jnp.float32)[:, None]
    return jnp.concatenate([weights * jnp.cos(phase), -weights * jnp.sin(phase)], axis=0).astype(jnp.bfloat16)

def whiten(ordered, taps, gap_mask):
    station_count = ordered.shape[0]
    pieces = ordered.reshape(station_count, NSEG, SEG).astype(jnp.float32)
    scaled = pieces * lax.rsqrt(lax.optimization_barrier(jnp.mean(pieces * pieces, axis=2, keepdims=True)) + 1e-06)
    normed = scaled.astype(jnp.bfloat16)
    spectrum = jnp.dot(normed.reshape(station_count * NSEG, SEG), forward_table(SEG), preferred_element_type=jnp.float32)
    spectrum = spectrum.reshape(station_count, NSEG, SEG)
    response = jnp.dot(taps, forward_table(TAPS), preferred_element_type=jnp.float32)[:, None, :]
    half_bins = SEG // 2
    spec_re = spectrum[:, :, :half_bins]
    spec_im = spectrum[:, :, half_bins:]
    resp_re = response[:, :, :half_bins]
    resp_im = response[:, :, half_bins:]
    weight = gap_mask.astype(jnp.float32)[:, :, None]
    white_re = (spec_re * resp_re - spec_im * resp_im) * weight
    white_im = (spec_re * resp_im + spec_im * resp_re) * weight
    return jnp.concatenate([white_re, white_im], axis=2).astype(jnp.bfloat16)

def pair_block(own_spec, own_mask, far_spec, far_mask, inverse):
    half_bins = SEG // 2
    highest = lax.Precision.HIGHEST
    own_full = own_spec.astype(jnp.float32)
    far_full = far_spec.astype(jnp.float32)
    own_re = own_full[:, :, :half_bins]
    own_im = own_full[:, :, half_bins:]
    far_re = far_full[:, :, :half_bins]
    far_im = far_full[:, :, half_bins:]
    cross_re = jnp.einsum('igk,jgk->kij', own_re, far_re, precision=highest) + jnp.einsum('igk,jgk->kij', own_im, far_im, precision=highest)
    cross_im = jnp.einsum('igk,jgk->kij', own_re, far_im, precision=highest) - jnp.einsum('igk,jgk->kij', own_im, far_re, precision=highest)
    cross_terms = jnp.concatenate([cross_re, cross_im], axis=0).astype(jnp.bfloat16)
    cross_terms = lax.optimization_barrier(cross_terms).astype(jnp.float32)
    summed = jnp.einsum('kij,kt->ijt', cross_terms, inverse.astype(jnp.float32), precision=highest)
    counts = jnp.dot(own_mask.astype(jnp.float32), far_mask.astype(jnp.float32).T, precision=highest)
    return (summed / (math.sqrt(SEG) * jnp.maximum(counts, 1.0))[:, :, None]).astype(jnp.bfloat16)

def reference(records, record_station, taps, gap_mask, partners):
    ordered = jnp.zeros_like(records).at[record_station].set(records)
    spectra = whiten(ordered, taps, gap_mask)
    inverse = inverse_table()
    block_total = STATIONS // SPB
    results = []
    for round_index in range(ROUNDS):

        def one_block(block_index, round_index=round_index):
            partner = partners[round_index, block_index].astype(jnp.int32)
            own_spec = lax.dynamic_slice_in_dim(spectra, (block_index * SPB).astype(jnp.int32), SPB, 0)
            own_mask = lax.dynamic_slice_in_dim(gap_mask, (block_index * SPB).astype(jnp.int32), SPB, 0)
            far_spec = lax.dynamic_slice_in_dim(spectra, (partner * SPB).astype(jnp.int32), SPB, 0)
            far_mask = lax.dynamic_slice_in_dim(gap_mask, (partner * SPB).astype(jnp.int32), SPB, 0)
            return pair_block(own_spec, own_mask, far_spec, far_mask, inverse)
        stacked = lax.map(one_block, jnp.arange(block_total, dtype=jnp.int32))
        results.append(stacked.reshape(STATIONS, SPB, SEG))
    return jnp.stack(results)
```

```python
import functools
import math

import jax
import jax.numpy as jnp
from jax import lax
from jax.sharding import PartitionSpec as P

SEG = 512
TAPS = 255
NSEG = 4


def angle_table(row_count, col_count):
    first = jnp.arange(row_count, dtype=jnp.int32)[:, None]
    second = jnp.arange(col_count, dtype=jnp.int32)[None, :]
    return 2.0 * math.pi / SEG * (first * second % SEG).astype(jnp.float32)


def forward_table(row_count):
    phase = angle_table(row_count, SEG // 2)
    return jnp.concatenate([jnp.cos(phase), -jnp.sin(phase)], axis=1).astype(jnp.bfloat16)


def inverse_table():
    phase = angle_table(SEG // 2, SEG)
    weights = jnp.where(jnp.arange(SEG // 2, dtype=jnp.int32) == 0, 1.0, 2.0).astype(jnp.float32)[
        :, None
    ]
    return jnp.concatenate([weights * jnp.cos(phase), -weights * jnp.sin(phase)], axis=0).astype(
        jnp.bfloat16
    )


def whiten(ordered, taps, gap_mask):
    station_count = ordered.shape[0]
    pieces = ordered.reshape(station_count, NSEG, SEG).astype(jnp.float32)
    scaled = pieces * lax.rsqrt(jnp.mean(pieces * pieces, axis=2, keepdims=True) + 1e-06)
    normed = scaled.astype(jnp.bfloat16)
    spectrum = jnp.dot(
        normed.reshape(station_count * NSEG, SEG),
        forward_table(SEG),
        preferred_element_type=jnp.float32,
    )
    spectrum = spectrum.reshape(station_count, NSEG, SEG)
    response = jnp.dot(taps, forward_table(TAPS), preferred_element_type=jnp.float32)[:, None, :]
    half_bins = SEG // 2
    spec_re = spectrum[:, :, :half_bins]
    spec_im = spectrum[:, :, half_bins:]
    resp_re = response[:, :, :half_bins]
    resp_im = response[:, :, half_bins:]
    weight = gap_mask.astype(jnp.float32)[:, :, None]
    white_re = (spec_re * resp_re - spec_im * resp_im) * weight
    white_im = (spec_re * resp_im + spec_im * resp_re) * weight
    return jnp.concatenate([white_re, white_im], axis=2).astype(jnp.bfloat16)


def place_records(records, record_station, per_block, block_total, my_index):
    owners = record_station // per_block
    label = (record_station - owners * per_block + 1).astype(records.dtype)
    tagged = jnp.concatenate(
        [records, jnp.broadcast_to(label[:, None], (records.shape[0], 128))], axis=1
    )
    outgoing = jnp.zeros((block_total, tagged.shape[1]), records.dtype).at[owners].set(tagged)
    arrived = lax.all_to_all(outgoing, "dev", split_axis=0, concat_axis=0, tiled=True)
    local_rows = arrived[:, records.shape[1]].astype(jnp.int32) - 1
    local_rows = jnp.where(local_rows >= 0, local_rows, per_block)
    return (
        jnp.zeros((per_block, records.shape[1]), records.dtype)
        .at[local_rows]
        .set(arrived[:, : records.shape[1]], mode="drop")
    )


def exchange(payload, code, device_total):
    levels = device_total.bit_length() - 1
    groups = [(0, min(3, levels))]
    while groups[-1][0] + groups[-1][1] < levels:
        shift = groups[-1][0] + groups[-1][1]
        groups.append((shift, min(2, levels - shift)))

    def send(mask, value):
        pairs = [(source, source ^ mask) for source in range(device_total)]
        return lax.ppermute(value, "dev", pairs)

    for shift, width in groups:
        part = jnp.bitwise_and(jnp.right_shift(code, shift), 2**width - 1)
        branches = [lambda value: value] + [
            functools.partial(send, step << shift) for step in range(1, 2**width)
        ]
        payload = lax.switch(part, branches, payload)
    return payload


def pair_block(own_spec, own_mask, far_spec, far_mask, inverse):
    half_bins = SEG // 2
    own_re = own_spec[:, :, :half_bins]
    own_im = own_spec[:, :, half_bins:]
    far_re = far_spec[:, :, :half_bins]
    far_im = far_spec[:, :, half_bins:]
    own_parts = jnp.concatenate([own_re, own_im], axis=1)
    far_parts = jnp.concatenate(
        [jnp.concatenate([far_re, far_im], axis=1), jnp.concatenate([far_im, -far_re], axis=1)],
        axis=0,
    )
    cross_terms = jnp.einsum(
        "igk,jgk->kij", own_parts, far_parts, preferred_element_type=jnp.float32
    )
    far_width = far_spec.shape[0]
    stacked = jnp.concatenate(
        [cross_terms[:, :, :far_width], cross_terms[:, :, far_width:]], axis=0
    ).astype(jnp.bfloat16)
    summed = jnp.einsum("kij,kt->ijt", stacked, inverse, preferred_element_type=jnp.float32)
    counts = jnp.dot(own_mask.astype(jnp.float32), far_mask.astype(jnp.float32).T)
    return (summed / (math.sqrt(SEG) * jnp.maximum(counts, 1.0))[:, :, None]).astype(jnp.bfloat16)


def shards(records, record_station, taps, gap_mask, partners):
    per_block = taps.shape[0]
    block_total = lax.axis_size("dev")
    my_index = lax.axis_index("dev")
    ordered = place_records(records, record_station, per_block, block_total, my_index)
    own_spec = whiten(ordered, taps, gap_mask)
    mask_row = jnp.zeros((1, SEG), jnp.bfloat16).at[0, : per_block * NSEG].set(
        gap_mask.reshape(-1).astype(jnp.bfloat16)
    )
    payload = jnp.concatenate([own_spec.reshape(per_block * NSEG, SEG), mask_row], axis=0)
    rounds = partners.shape[0]
    codes = jnp.bitwise_xor(my_index, partners[:, my_index])

    def fetch(round_index, gathered):
        arrived = exchange(payload, codes[round_index], block_total)
        return lax.dynamic_update_index_in_dim(gathered, arrived, round_index, 0)

    gathered = lax.fori_loop(
        0, rounds, fetch, jnp.zeros((rounds,) + payload.shape, payload.dtype)
    )
    inverse = inverse_table()
    outputs = []
    for round_index in range(rounds):
        arrived = gathered[round_index]
        far_spec = arrived[: per_block * NSEG].reshape(per_block, NSEG, SEG)
        far_mask = arrived[per_block * NSEG, : per_block * NSEG].reshape(per_block, NSEG)
        outputs.append(pair_block(own_spec, gap_mask, far_spec, far_mask, inverse))
    return jnp.stack(outputs)


def solution(mesh):
    in_specs = (P("dev", None), P("dev"), P("dev", None), P("dev", None), P())
    out_specs = P(None, "dev", None, None)
    return jax.shard_map(shards, mesh=mesh, in_specs=in_specs, out_specs=out_specs, check_vma=False)
```

```python
import functools
import math

import jax
import jax.numpy as jnp
from jax import lax
from jax.experimental import pallas as pl
from jax.experimental.pallas import tpu as pltpu
from jax.sharding import PartitionSpec as P

SEG = 512
H = SEG // 2
TAPS = 255
NSEG = 4


def angle_table(row_count, col_count):
    first = jnp.arange(row_count, dtype=jnp.int32)[:, None]
    second = jnp.arange(col_count, dtype=jnp.int32)[None, :]
    return 2.0 * math.pi / SEG * (first * second % SEG).astype(jnp.float32)


def forward_table(row_count):
    phase = angle_table(row_count, SEG // 2)
    return jnp.concatenate([jnp.cos(phase), -jnp.sin(phase)], axis=1).astype(jnp.bfloat16)


def inverse_table():
    phase = angle_table(SEG // 2, SEG)
    weights = jnp.where(jnp.arange(SEG // 2, dtype=jnp.int32) == 0, 1.0, 2.0).astype(jnp.float32)[
        :, None
    ]
    return jnp.concatenate([weights * jnp.cos(phase), -weights * jnp.sin(phase)], axis=0).astype(
        jnp.bfloat16
    )


def whiten(ordered, taps, gap_mask):
    station_count = ordered.shape[0]
    pieces = ordered.reshape(station_count, NSEG, SEG).astype(jnp.float32)
    scaled = pieces * lax.rsqrt(jnp.mean(pieces * pieces, axis=2, keepdims=True) + 1e-06)
    normed = scaled.astype(jnp.bfloat16)
    spectrum = jnp.dot(
        normed.reshape(station_count * NSEG, SEG),
        forward_table(SEG),
        preferred_element_type=jnp.float32,
    )
    spectrum = spectrum.reshape(station_count, NSEG, SEG)
    response = jnp.dot(taps, forward_table(TAPS), preferred_element_type=jnp.float32)[:, None, :]
    half_bins = SEG // 2
    spec_re = spectrum[:, :, :half_bins]
    spec_im = spectrum[:, :, half_bins:]
    resp_re = response[:, :, :half_bins]
    resp_im = response[:, :, half_bins:]
    weight = gap_mask.astype(jnp.float32)[:, :, None]
    white_re = (spec_re * resp_re - spec_im * resp_im) * weight
    white_im = (spec_re * resp_im + spec_im * resp_re) * weight
    return jnp.concatenate([white_re, white_im], axis=2).astype(jnp.bfloat16)


def place_records(records, record_station, per_block, block_total, my_index):
    owners = record_station // per_block
    label = (record_station - owners * per_block + 1).astype(records.dtype)
    tagged = jnp.concatenate(
        [records, jnp.broadcast_to(label[:, None], (records.shape[0], 128))], axis=1
    )
    outgoing = jnp.zeros((block_total, tagged.shape[1]), records.dtype).at[owners].set(tagged)
    arrived = lax.all_to_all(outgoing, "dev", split_axis=0, concat_axis=0, tiled=True)
    local_rows = arrived[:, records.shape[1]].astype(jnp.int32) - 1
    local_rows = jnp.where(local_rows >= 0, local_rows, per_block)
    return (
        jnp.zeros((per_block, records.shape[1]), records.dtype)
        .at[local_rows]
        .set(arrived[:, : records.shape[1]], mode="drop")
    )


def exchange(payload, code, device_total):
    levels = device_total.bit_length() - 1
    groups = [(0, min(3, levels))]
    while groups[-1][0] + groups[-1][1] < levels:
        shift = groups[-1][0] + groups[-1][1]
        groups.append((shift, min(2, levels - shift)))

    def send(mask, value):
        pairs = [(source, source ^ mask) for source in range(device_total)]
        return lax.ppermute(value, "dev", pairs)

    for shift, width in groups:
        part = jnp.bitwise_and(jnp.right_shift(code, shift), 2**width - 1)
        branches = [lambda value: value] + [
            functools.partial(send, step << shift) for step in range(1, 2**width)
        ]
        payload = lax.switch(part, branches, payload)
    return payload


def cross_kernel(own_ref, far_ref, out_ref, planes, *, rows, chunk):
    planes[...] = far_ref[0].astype(jnp.float32)

    def one(i, carry):
        own = own_ref[i].astype(jnp.float32)
        for start in range(0, planes.shape[1], chunk):
            cut = pl.ds(start, chunk)
            acc_re = jnp.zeros((chunk, H), jnp.float32)
            acc_im = jnp.zeros((chunk, H), jnp.float32)
            for g in range(4):
                a_re = own[g : g + 1, :]
                a_im = own[4 + g : 5 + g, :]
                b_re = planes[g, cut, :]
                b_im = planes[4 + g, cut, :]
                acc_re = acc_re + a_re * b_re + a_im * b_im
                acc_im = acc_im + a_re * b_im - a_im * b_re
            out_ref[0, i, cut, 0:H] = acc_re.astype(out_ref.dtype)
            out_ref[0, i, cut, H:SEG] = acc_im.astype(out_ref.dtype)
        return carry

    lax.fori_loop(0, rows, one, 0)


def cross_spectra(own_parts, far_planes, rows=8, chunk=16):
    stations = own_parts.shape[0]
    rounds, parts, far_stations, bins = far_planes.shape
    return pl.pallas_call(
        functools.partial(cross_kernel, rows=rows, chunk=chunk),
        grid=(rounds, stations // rows),
        in_specs=[
            pl.BlockSpec((rows, parts, bins), lambda r, b: (b, 0, 0)),
            pl.BlockSpec((1, parts, far_stations, bins), lambda r, b: (r, 0, 0, 0)),
        ],
        out_specs=pl.BlockSpec((1, rows, far_stations, 2 * bins), lambda r, b: (r, b, 0, 0)),
        out_shape=jax.ShapeDtypeStruct((rounds, stations, far_stations, 2 * bins), jnp.bfloat16),
        scratch_shapes=[pltpu.VMEM((parts, far_stations, bins), jnp.float32)],
    )(own_parts, far_planes)


def shards(records, record_station, taps, gap_mask, partners):
    per_block = taps.shape[0]
    block_total = lax.axis_size("dev")
    my_index = lax.axis_index("dev")
    ordered = place_records(records, record_station, per_block, block_total, my_index)
    own_spec = whiten(ordered, taps, gap_mask)
    mask_row = jnp.zeros((1, SEG), jnp.bfloat16).at[0, : per_block * NSEG].set(
        gap_mask.reshape(-1).astype(jnp.bfloat16)
    )
    payload = jnp.concatenate([own_spec.reshape(per_block * NSEG, SEG), mask_row], axis=0)
    rounds = partners.shape[0]
    codes = jnp.bitwise_xor(my_index, partners[:, my_index])

    def fetch(round_index, gathered):
        arrived = exchange(payload, codes[round_index], block_total)
        return lax.dynamic_update_index_in_dim(gathered, arrived, round_index, 0)

    gathered = lax.fori_loop(
        0, rounds, fetch, jnp.zeros((rounds,) + payload.shape, payload.dtype)
    )
    far = gathered[:, : per_block * NSEG].reshape(rounds, per_block, NSEG, SEG)
    far_masks = gathered[:, per_block * NSEG, : per_block * NSEG].reshape(rounds, per_block, NSEG)
    own_parts = jnp.concatenate([own_spec[..., :H], own_spec[..., H:]], axis=1)
    far_planes = jnp.concatenate([far[..., :H], far[..., H:]], axis=2).transpose(0, 2, 1, 3)
    cross = cross_spectra(own_parts, far_planes, rows=16, chunk=32)
    summed = jnp.einsum("rijk,kt->rijt", cross, inverse_table(), preferred_element_type=jnp.float32)
    counts = jnp.einsum("ig,rjg->rij", gap_mask.astype(jnp.float32), far_masks.astype(jnp.float32))
    scale = 1.0 / (math.sqrt(SEG) * jnp.maximum(counts, 1.0))
    return (summed * scale[..., None]).astype(jnp.bfloat16)


def solution(mesh):
    in_specs = (P("dev", None), P("dev"), P("dev", None), P("dev", None), P())
    out_specs = P(None, "dev", None, None)
    return jax.shard_map(shards, mesh=mesh, in_specs=in_specs, out_specs=out_specs, check_vma=False)
```

```python
import functools
import math

import jax
import jax.numpy as jnp
from jax import lax
from jax.experimental import pallas as pl
from jax.experimental.pallas import tpu as pltpu
from jax.sharding import PartitionSpec as P

SEG = 512
H = SEG // 2
TAPS = 255
NSEG = 4


def angle_table(row_count, col_count):
    first = jnp.arange(row_count, dtype=jnp.int32)[:, None]
    second = jnp.arange(col_count, dtype=jnp.int32)[None, :]
    return 2.0 * math.pi / SEG * (first * second % SEG).astype(jnp.float32)


def forward_table(row_count):
    phase = angle_table(row_count, SEG // 2)
    return jnp.concatenate([jnp.cos(phase), -jnp.sin(phase)], axis=1).astype(jnp.bfloat16)


def inverse_table():
    phase = angle_table(SEG // 2, SEG)
    weights = jnp.where(jnp.arange(SEG // 2, dtype=jnp.int32) == 0, 1.0, 2.0).astype(jnp.float32)[
        :, None
    ]
    return jnp.concatenate([weights * jnp.cos(phase), -weights * jnp.sin(phase)], axis=0).astype(
        jnp.bfloat16
    )


def whiten(ordered, taps, gap_mask):
    station_count = ordered.shape[0]
    pieces = ordered.reshape(station_count, NSEG, SEG).astype(jnp.float32)
    scaled = pieces * lax.rsqrt(jnp.mean(pieces * pieces, axis=2, keepdims=True) + 1e-06)
    normed = scaled.astype(jnp.bfloat16)
    spectrum = jnp.dot(
        normed.reshape(station_count * NSEG, SEG),
        forward_table(SEG),
        preferred_element_type=jnp.float32,
    )
    spectrum = spectrum.reshape(station_count, NSEG, SEG)
    response = jnp.dot(taps, forward_table(TAPS), preferred_element_type=jnp.float32)[:, None, :]
    half_bins = SEG // 2
    spec_re = spectrum[:, :, :half_bins]
    spec_im = spectrum[:, :, half_bins:]
    resp_re = response[:, :, :half_bins]
    resp_im = response[:, :, half_bins:]
    weight = gap_mask.astype(jnp.float32)[:, :, None]
    white_re = (spec_re * resp_re - spec_im * resp_im) * weight
    white_im = (spec_re * resp_im + spec_im * resp_re) * weight
    return jnp.concatenate([white_re, white_im], axis=2).astype(jnp.bfloat16)


def place_records(records, record_station, per_block, block_total, my_index):
    owners = record_station // per_block
    label = (record_station - owners * per_block + 1).astype(records.dtype)
    tagged = jnp.concatenate(
        [records, jnp.broadcast_to(label[:, None], (records.shape[0], 128))], axis=1
    )
    outgoing = jnp.zeros((block_total, tagged.shape[1]), records.dtype).at[owners].set(tagged)
    arrived = lax.all_to_all(outgoing, "dev", split_axis=0, concat_axis=0, tiled=True)
    local_rows = arrived[:, records.shape[1]].astype(jnp.int32) - 1
    local_rows = jnp.where(local_rows >= 0, local_rows, per_block)
    return (
        jnp.zeros((per_block, records.shape[1]), records.dtype)
        .at[local_rows]
        .set(arrived[:, : records.shape[1]], mode="drop")
    )


def exchange(payload, code, device_total):
    levels = device_total.bit_length() - 1
    groups = [(0, min(3, levels))]
    if levels > 3:
        groups.append((3, levels - 3))

    def send(mask, value):
        pairs = [(source, source ^ mask) for source in range(device_total)]
        return lax.ppermute(value, "dev", pairs)

    for shift, width in groups:
        part = jnp.bitwise_and(jnp.right_shift(code, shift), 2**width - 1)
        branches = [lambda value: value] + [
            functools.partial(send, step << shift) for step in range(1, 2**width)
        ]
        payload = lax.switch(part, branches, payload)
    return payload


def cross_kernel(own_ref, far_ref, out_ref, planes, *, rows, chunk):
    planes[...] = far_ref[0].astype(jnp.float32)

    def one(i, carry):
        own = own_ref[i].astype(jnp.float32)
        for start in range(0, planes.shape[1], chunk):
            cut = pl.ds(start, chunk)
            acc_re = jnp.zeros((chunk, H), jnp.float32)
            acc_im = jnp.zeros((chunk, H), jnp.float32)
            for g in range(4):
                a_re = own[g : g + 1, :]
                a_im = own[4 + g : 5 + g, :]
                b_re = planes[g, cut, :]
                b_im = planes[4 + g, cut, :]
                acc_re = acc_re + a_re * b_re + a_im * b_im
                acc_im = acc_im + a_re * b_im - a_im * b_re
            out_ref[0, i, cut, 0:H] = acc_re.astype(out_ref.dtype)
            out_ref[0, i, cut, H:SEG] = acc_im.astype(out_ref.dtype)
        return carry

    lax.fori_loop(0, rows, one, 0)


def cross_spectra(own_parts, far_planes, rows=8, chunk=16):
    stations = own_parts.shape[0]
    rounds, parts, far_stations, bins = far_planes.shape
    return pl.pallas_call(
        functools.partial(cross_kernel, rows=rows, chunk=chunk),
        grid=(rounds, stations // rows),
        in_specs=[
            pl.BlockSpec((rows, parts, bins), lambda r, b: (b, 0, 0)),
            pl.BlockSpec((1, parts, far_stations, bins), lambda r, b: (r, 0, 0, 0)),
        ],
        out_specs=pl.BlockSpec((1, rows, far_stations, 2 * bins), lambda r, b: (r, b, 0, 0)),
        out_shape=jax.ShapeDtypeStruct((rounds, stations, far_stations, 2 * bins), jnp.bfloat16),
        scratch_shapes=[pltpu.VMEM((parts, far_stations, bins), jnp.float32)],
    )(own_parts, far_planes)


def shards(records, record_station, taps, gap_mask, partners):
    per_block = taps.shape[0]
    block_total = lax.axis_size("dev")
    my_index = lax.axis_index("dev")
    ordered = place_records(records, record_station, per_block, block_total, my_index)
    own_spec = whiten(ordered, taps, gap_mask)
    mask_row = jnp.zeros((1, SEG), jnp.bfloat16).at[0, : per_block * NSEG].set(
        gap_mask.reshape(-1).astype(jnp.bfloat16)
    )
    payload = jnp.concatenate([own_spec.reshape(per_block * NSEG, SEG), mask_row], axis=0)
    rounds = partners.shape[0]
    codes = jnp.bitwise_xor(my_index, partners[:, my_index])

    def fetch(round_index, gathered):
        arrived = exchange(payload, codes[round_index], block_total)
        return lax.dynamic_update_index_in_dim(gathered, arrived, round_index, 0)

    gathered = lax.fori_loop(
        0, rounds, fetch, jnp.zeros((rounds,) + payload.shape, payload.dtype)
    )
    far = gathered[:, : per_block * NSEG].reshape(rounds, per_block, NSEG, SEG)
    far_masks = gathered[:, per_block * NSEG, : per_block * NSEG].reshape(rounds, per_block, NSEG)
    own_parts = jnp.concatenate([own_spec[..., :H], own_spec[..., H:]], axis=1)
    far_planes = jnp.concatenate([far[..., :H], far[..., H:]], axis=2).transpose(0, 2, 1, 3)
    cross = cross_spectra(own_parts, far_planes, rows=16, chunk=32)
    summed = jnp.einsum("rijk,kt->rijt", cross, inverse_table(), preferred_element_type=jnp.float32)
    counts = jnp.einsum("ig,rjg->rij", gap_mask.astype(jnp.float32), far_masks.astype(jnp.float32))
    scale = 1.0 / (math.sqrt(SEG) * jnp.maximum(counts, 1.0))
    return (summed * scale[..., None]).astype(jnp.bfloat16)


def solution(mesh):
    in_specs = (P("dev", None), P("dev"), P("dev", None), P("dev", None), P())
    out_specs = P(None, "dev", None, None)
    return jax.shard_map(shards, mesh=mesh, in_specs=in_specs, out_specs=out_specs, check_vma=False)
```

```python
import functools
import math

import jax
import jax.numpy as jnp
from jax import lax
from jax.experimental import pallas as pl
from jax.experimental.pallas import tpu as pltpu
from jax.sharding import PartitionSpec as P

SEG = 512
H = SEG // 2
TAPS = 255
NSEG = 4


def angle_table(row_count, col_count):
    first = jnp.arange(row_count, dtype=jnp.int32)[:, None]
    second = jnp.arange(col_count, dtype=jnp.int32)[None, :]
    return 2.0 * math.pi / SEG * (first * second % SEG).astype(jnp.float32)


def forward_table(row_count):
    phase = angle_table(row_count, SEG // 2)
    return jnp.concatenate([jnp.cos(phase), -jnp.sin(phase)], axis=1).astype(jnp.bfloat16)


def inverse_table():
    phase = angle_table(SEG // 2, SEG)
    weights = jnp.where(jnp.arange(SEG // 2, dtype=jnp.int32) == 0, 1.0, 2.0).astype(jnp.float32)[
        :, None
    ]
    return jnp.concatenate([weights * jnp.cos(phase), -weights * jnp.sin(phase)], axis=0).astype(
        jnp.bfloat16
    )


def whiten(ordered, taps, gap_mask):
    station_count = ordered.shape[0]
    pieces = ordered.reshape(station_count, NSEG, SEG).astype(jnp.float32)
    scaled = pieces * lax.rsqrt(jnp.mean(pieces * pieces, axis=2, keepdims=True) + 1e-06)
    normed = scaled.astype(jnp.bfloat16)
    spectrum = jnp.dot(
        normed.reshape(station_count * NSEG, SEG),
        forward_table(SEG),
        preferred_element_type=jnp.float32,
    )
    spectrum = spectrum.reshape(station_count, NSEG, SEG)
    response = jnp.dot(taps, forward_table(TAPS), preferred_element_type=jnp.float32)[:, None, :]
    half_bins = SEG // 2
    spec_re = spectrum[:, :, :half_bins]
    spec_im = spectrum[:, :, half_bins:]
    resp_re = response[:, :, :half_bins]
    resp_im = response[:, :, half_bins:]
    weight = gap_mask.astype(jnp.float32)[:, :, None]
    white_re = (spec_re * resp_re - spec_im * resp_im) * weight
    white_im = (spec_re * resp_im + spec_im * resp_re) * weight
    return jnp.concatenate([white_re, white_im], axis=2).astype(jnp.bfloat16)


def place_records(records, record_station, per_block, block_total, my_index):
    owners = record_station // per_block
    label = (record_station - owners * per_block + 1).astype(records.dtype)
    tagged = jnp.concatenate(
        [records, jnp.broadcast_to(label[:, None], (records.shape[0], 128))], axis=1
    )
    outgoing = jnp.zeros((block_total, tagged.shape[1]), records.dtype).at[owners].set(tagged)
    arrived = lax.all_to_all(outgoing, "dev", split_axis=0, concat_axis=0, tiled=True)
    local_rows = arrived[:, records.shape[1]].astype(jnp.int32) - 1
    local_rows = jnp.where(local_rows >= 0, local_rows, per_block)
    return (
        jnp.zeros((per_block, records.shape[1]), records.dtype)
        .at[local_rows]
        .set(arrived[:, : records.shape[1]], mode="drop")
    )


def exchange(payload, code, device_total):
    levels = device_total.bit_length() - 1
    groups = [(0, levels)]

    def send(mask, value):
        pairs = [(source, source ^ mask) for source in range(device_total)]
        return lax.ppermute(value, "dev", pairs)

    for shift, width in groups:
        part = jnp.bitwise_and(jnp.right_shift(code, shift), 2**width - 1)
        branches = [lambda value: value] + [
            functools.partial(send, step << shift) for step in range(1, 2**width)
        ]
        payload = lax.switch(part, branches, payload)
    return payload


def cross_kernel(own_ref, far_ref, out_ref, planes, *, rows, chunk):
    planes[...] = far_ref[0].astype(jnp.float32)

    def one(i, carry):
        own = own_ref[i].astype(jnp.float32)
        for start in range(0, planes.shape[1], chunk):
            cut = pl.ds(start, chunk)
            acc_re = jnp.zeros((chunk, H), jnp.float32)
            acc_im = jnp.zeros((chunk, H), jnp.float32)
            for g in range(4):
                a_re = own[g : g + 1, :]
                a_im = own[4 + g : 5 + g, :]
                b_re = planes[g, cut, :]
                b_im = planes[4 + g, cut, :]
                acc_re = acc_re + a_re * b_re + a_im * b_im
                acc_im = acc_im + a_re * b_im - a_im * b_re
            out_ref[0, i, cut, 0:H] = acc_re.astype(out_ref.dtype)
            out_ref[0, i, cut, H:SEG] = acc_im.astype(out_ref.dtype)
        return carry

    lax.fori_loop(0, rows, one, 0)


def cross_spectra(own_parts, far_planes, rows=8, chunk=16):
    stations = own_parts.shape[0]
    rounds, parts, far_stations, bins = far_planes.shape
    return pl.pallas_call(
        functools.partial(cross_kernel, rows=rows, chunk=chunk),
        grid=(rounds, stations // rows),
        in_specs=[
            pl.BlockSpec((rows, parts, bins), lambda r, b: (b, 0, 0)),
            pl.BlockSpec((1, parts, far_stations, bins), lambda r, b: (r, 0, 0, 0)),
        ],
        out_specs=pl.BlockSpec((1, rows, far_stations, 2 * bins), lambda r, b: (r, b, 0, 0)),
        out_shape=jax.ShapeDtypeStruct((rounds, stations, far_stations, 2 * bins), jnp.bfloat16),
        scratch_shapes=[pltpu.VMEM((parts, far_stations, bins), jnp.float32)],
    )(own_parts, far_planes)


def shards(records, record_station, taps, gap_mask, partners):
    per_block = taps.shape[0]
    block_total = lax.axis_size("dev")
    my_index = lax.axis_index("dev")
    ordered = place_records(records, record_station, per_block, block_total, my_index)
    own_spec = whiten(ordered, taps, gap_mask)
    mask_row = jnp.zeros((1, SEG), jnp.bfloat16).at[0, : per_block * NSEG].set(
        gap_mask.reshape(-1).astype(jnp.bfloat16)
    )
    payload = jnp.concatenate([own_spec.reshape(per_block * NSEG, SEG), mask_row], axis=0)
    rounds = partners.shape[0]
    codes = jnp.bitwise_xor(my_index, partners[:, my_index])

    def fetch(round_index, gathered):
        arrived = exchange(payload, codes[round_index], block_total)
        return lax.dynamic_update_index_in_dim(gathered, arrived, round_index, 0)

    gathered = lax.fori_loop(
        0, rounds, fetch, jnp.zeros((rounds,) + payload.shape, payload.dtype)
    )
    far = gathered[:, : per_block * NSEG].reshape(rounds, per_block, NSEG, SEG)
    far_masks = gathered[:, per_block * NSEG, : per_block * NSEG].reshape(rounds, per_block, NSEG)
    own_parts = jnp.concatenate([own_spec[..., :H], own_spec[..., H:]], axis=1)
    far_planes = jnp.concatenate([far[..., :H], far[..., H:]], axis=2).transpose(0, 2, 1, 3)
    cross = cross_spectra(own_parts, far_planes, rows=16, chunk=32)
    summed = jnp.einsum("rijk,kt->rijt", cross, inverse_table(), preferred_element_type=jnp.float32)
    counts = jnp.einsum("ig,rjg->rij", gap_mask.astype(jnp.float32), far_masks.astype(jnp.float32))
    scale = 1.0 / (math.sqrt(SEG) * jnp.maximum(counts, 1.0))
    return (summed * scale[..., None]).astype(jnp.bfloat16)


def solution(mesh):
    in_specs = (P("dev", None), P("dev"), P("dev", None), P("dev", None), P())
    out_specs = P(None, "dev", None, None)
    return jax.shard_map(shards, mesh=mesh, in_specs=in_specs, out_specs=out_specs, check_vma=False)
```

```python
import functools
import math

import jax
import jax.numpy as jnp
from jax import lax
from jax.experimental import pallas as pl
from jax.experimental.pallas import tpu as pltpu
from jax.sharding import PartitionSpec as P

SEG = 512
H = SEG // 2
TAPS = 255
NSEG = 4


def angle_table(row_count, col_count):
    first = jnp.arange(row_count, dtype=jnp.int32)[:, None]
    second = jnp.arange(col_count, dtype=jnp.int32)[None, :]
    return 2.0 * math.pi / SEG * (first * second % SEG).astype(jnp.float32)


def forward_table(row_count):
    phase = angle_table(row_count, SEG // 2)
    return jnp.concatenate([jnp.cos(phase), -jnp.sin(phase)], axis=1).astype(jnp.bfloat16)


def inverse_table():
    phase = angle_table(SEG // 2, SEG)
    weights = jnp.where(jnp.arange(SEG // 2, dtype=jnp.int32) == 0, 1.0, 2.0).astype(jnp.float32)[
        :, None
    ]
    return jnp.concatenate([weights * jnp.cos(phase), -weights * jnp.sin(phase)], axis=0).astype(
        jnp.bfloat16
    )


def whiten(ordered, taps, gap_mask):
    station_count = ordered.shape[0]
    pieces = ordered.reshape(station_count, NSEG, SEG).astype(jnp.float32)
    scaled = pieces * lax.rsqrt(jnp.mean(pieces * pieces, axis=2, keepdims=True) + 1e-06)
    normed = scaled.astype(jnp.bfloat16)
    spectrum = jnp.dot(
        normed.reshape(station_count * NSEG, SEG),
        forward_table(SEG),
        preferred_element_type=jnp.float32,
    )
    spectrum = spectrum.reshape(station_count, NSEG, SEG)
    response = jnp.dot(taps, forward_table(TAPS), preferred_element_type=jnp.float32)[:, None, :]
    half_bins = SEG // 2
    spec_re = spectrum[:, :, :half_bins]
    spec_im = spectrum[:, :, half_bins:]
    resp_re = response[:, :, :half_bins]
    resp_im = response[:, :, half_bins:]
    weight = gap_mask.astype(jnp.float32)[:, :, None]
    white_re = (spec_re * resp_re - spec_im * resp_im) * weight
    white_im = (spec_re * resp_im + spec_im * resp_re) * weight
    return jnp.concatenate([white_re, white_im], axis=2).astype(jnp.bfloat16)


def place_records(records, record_station, per_block, block_total, my_index):
    owners = record_station // per_block
    label = (record_station - owners * per_block + 1).astype(records.dtype)
    tagged = jnp.concatenate(
        [records, jnp.broadcast_to(label[:, None], (records.shape[0], 128))], axis=1
    )
    outgoing = jnp.zeros((block_total, tagged.shape[1]), records.dtype).at[owners].set(tagged)
    arrived = lax.all_to_all(outgoing, "dev", split_axis=0, concat_axis=0, tiled=True)
    local_rows = arrived[:, records.shape[1]].astype(jnp.int32) - 1
    local_rows = jnp.where(local_rows >= 0, local_rows, per_block)
    return (
        jnp.zeros((per_block, records.shape[1]), records.dtype)
        .at[local_rows]
        .set(arrived[:, : records.shape[1]], mode="drop")
    )


def exchange(payload, code, device_total):
    levels = device_total.bit_length() - 1
    groups = [(0, min(3, levels))]
    if levels > 3:
        groups.append((3, levels - 3))

    def send(mask, value):
        pairs = [(source, source ^ mask) for source in range(device_total)]
        return lax.ppermute(value, "dev", pairs)

    for shift, width in groups:
        part = jnp.bitwise_and(jnp.right_shift(code, shift), 2**width - 1)
        branches = [lambda value: value] + [
            functools.partial(send, step << shift) for step in range(1, 2**width)
        ]
        payload = lax.switch(part, branches, payload)
    return payload


def cross_kernel(own_ref, far_ref, out_ref, planes, *, rows, chunk):
    planes[...] = far_ref[0].astype(jnp.float32)

    def one(i, carry):
        own = own_ref[i].astype(jnp.float32)
        for start in range(0, planes.shape[1], chunk):
            cut = pl.ds(start, chunk)
            acc_re = jnp.zeros((chunk, H), jnp.float32)
            acc_im = jnp.zeros((chunk, H), jnp.float32)
            for g in range(4):
                a_re = own[g : g + 1, :]
                a_im = own[4 + g : 5 + g, :]
                b_re = planes[g, cut, :]
                b_im = planes[4 + g, cut, :]
                acc_re = acc_re + a_re * b_re + a_im * b_im
                acc_im = acc_im + a_re * b_im - a_im * b_re
            out_ref[0, i, cut, 0:H] = acc_re.astype(out_ref.dtype)
            out_ref[0, i, cut, H:SEG] = acc_im.astype(out_ref.dtype)
        return carry

    lax.fori_loop(0, rows, one, 0)


def cross_spectra(own_parts, far_planes, rows=8, chunk=16):
    stations = own_parts.shape[0]
    rounds, parts, far_stations, bins = far_planes.shape
    return pl.pallas_call(
        functools.partial(cross_kernel, rows=rows, chunk=chunk),
        grid=(rounds, stations // rows),
        in_specs=[
            pl.BlockSpec((rows, parts, bins), lambda r, b: (b, 0, 0)),
            pl.BlockSpec((1, parts, far_stations, bins), lambda r, b: (r, 0, 0, 0)),
        ],
        out_specs=pl.BlockSpec((1, rows, far_stations, 2 * bins), lambda r, b: (r, b, 0, 0)),
        out_shape=jax.ShapeDtypeStruct((rounds, stations, far_stations, 2 * bins), jnp.bfloat16),
        scratch_shapes=[pltpu.VMEM((parts, far_stations, bins), jnp.float32)],
    )(own_parts, far_planes)


def shards(records, record_station, taps, gap_mask, partners):
    per_block = taps.shape[0]
    block_total = lax.axis_size("dev")
    my_index = lax.axis_index("dev")
    ordered = place_records(records, record_station, per_block, block_total, my_index)
    own_spec = whiten(ordered, taps, gap_mask)
    mask_row = jnp.zeros((1, SEG), jnp.bfloat16).at[0, : per_block * NSEG].set(
        gap_mask.reshape(-1).astype(jnp.bfloat16)
    )
    payload = jnp.concatenate([own_spec.reshape(per_block * NSEG, SEG), mask_row], axis=0)
    half = per_block * NSEG // 2
    pieces = (payload[:half], payload[half:])
    rounds = partners.shape[0]
    codes = jnp.bitwise_xor(my_index, partners[:, my_index])

    def fetch(round_index, gathered):
        arrived = exchange(pieces, codes[round_index], block_total)
        return tuple(
            lax.dynamic_update_index_in_dim(kept, piece, round_index, 0)
            for kept, piece in zip(gathered, arrived)
        )

    gathered = lax.fori_loop(
        0,
        rounds,
        fetch,
        tuple(jnp.zeros((rounds,) + piece.shape, piece.dtype) for piece in pieces),
    )
    gathered = jnp.concatenate(gathered, axis=1)
    far = gathered[:, : per_block * NSEG].reshape(rounds, per_block, NSEG, SEG)
    far_masks = gathered[:, per_block * NSEG, : per_block * NSEG].reshape(rounds, per_block, NSEG)
    own_parts = jnp.concatenate([own_spec[..., :H], own_spec[..., H:]], axis=1)
    far_planes = jnp.concatenate([far[..., :H], far[..., H:]], axis=2).transpose(0, 2, 1, 3)
    cross = cross_spectra(own_parts, far_planes, rows=16, chunk=32)
    summed = jnp.einsum("rijk,kt->rijt", cross, inverse_table(), preferred_element_type=jnp.float32)
    counts = jnp.einsum("ig,rjg->rij", gap_mask.astype(jnp.float32), far_masks.astype(jnp.float32))
    scale = 1.0 / (math.sqrt(SEG) * jnp.maximum(counts, 1.0))
    return (summed * scale[..., None]).astype(jnp.bfloat16)


def solution(mesh):
    in_specs = (P("dev", None), P("dev"), P("dev", None), P("dev", None), P())
    out_specs = P(None, "dev", None, None)
    return jax.shard_map(shards, mesh=mesh, in_specs=in_specs, out_specs=out_specs, check_vma=False)
```

```python
import functools
import math

import jax
import jax.numpy as jnp
from jax import lax
from jax.experimental import pallas as pl
from jax.experimental.pallas import tpu as pltpu
from jax.sharding import PartitionSpec as P

SEG = 512
H = SEG // 2
TAPS = 255
NSEG = 4


def angle_table(row_count, col_count):
    first = jnp.arange(row_count, dtype=jnp.int32)[:, None]
    second = jnp.arange(col_count, dtype=jnp.int32)[None, :]
    return 2.0 * math.pi / SEG * (first * second % SEG).astype(jnp.float32)


def forward_table(row_count):
    phase = angle_table(row_count, SEG // 2)
    return jnp.concatenate([jnp.cos(phase), -jnp.sin(phase)], axis=1).astype(jnp.bfloat16)


def inverse_table():
    phase = angle_table(SEG // 2, SEG)
    weights = jnp.where(jnp.arange(SEG // 2, dtype=jnp.int32) == 0, 1.0, 2.0).astype(jnp.float32)[
        :, None
    ]
    return jnp.concatenate([weights * jnp.cos(phase), -weights * jnp.sin(phase)], axis=0).astype(
        jnp.bfloat16
    )


def whiten(ordered, taps, gap_mask):
    station_count = ordered.shape[0]
    pieces = ordered.reshape(station_count, NSEG, SEG).astype(jnp.float32)
    scaled = pieces * lax.rsqrt(jnp.mean(pieces * pieces, axis=2, keepdims=True) + 1e-06)
    normed = scaled.astype(jnp.bfloat16)
    spectrum = jnp.dot(
        normed.reshape(station_count * NSEG, SEG),
        forward_table(SEG),
        preferred_element_type=jnp.float32,
    )
    spectrum = spectrum.reshape(station_count, NSEG, SEG)
    response = jnp.dot(taps, forward_table(TAPS), preferred_element_type=jnp.float32)[:, None, :]
    half_bins = SEG // 2
    spec_re = spectrum[:, :, :half_bins]
    spec_im = spectrum[:, :, half_bins:]
    resp_re = response[:, :, :half_bins]
    resp_im = response[:, :, half_bins:]
    weight = gap_mask.astype(jnp.float32)[:, :, None]
    white_re = (spec_re * resp_re - spec_im * resp_im) * weight
    white_im = (spec_re * resp_im + spec_im * resp_re) * weight
    return jnp.concatenate([white_re, white_im], axis=2).astype(jnp.bfloat16)


def place_records(records, record_station, per_block, block_total, my_index):
    owners = record_station // per_block
    label = (record_station - owners * per_block + 1).astype(records.dtype)
    tagged = jnp.concatenate(
        [records, jnp.broadcast_to(label[:, None], (records.shape[0], 128))], axis=1
    )
    outgoing = jnp.zeros((block_total, tagged.shape[1]), records.dtype).at[owners].set(tagged)
    arrived = lax.all_to_all(outgoing, "dev", split_axis=0, concat_axis=0, tiled=True)
    local_rows = arrived[:, records.shape[1]].astype(jnp.int32) - 1
    local_rows = jnp.where(local_rows >= 0, local_rows, per_block)
    return (
        jnp.zeros((per_block, records.shape[1]), records.dtype)
        .at[local_rows]
        .set(arrived[:, : records.shape[1]], mode="drop")
    )


def exchange(payload, code, device_total):
    levels = device_total.bit_length() - 1
    groups = [(0, min(3, levels))]
    if levels > 3:
        groups.append((3, levels - 3))

    def send(mask, value):
        pairs = [(source, source ^ mask) for source in range(device_total)]
        return lax.ppermute(value, "dev", pairs)

    for shift, width in groups:
        part = jnp.bitwise_and(jnp.right_shift(code, shift), 2**width - 1)
        branches = [lambda value: value] + [
            functools.partial(send, step << shift) for step in range(1, 2**width)
        ]
        payload = lax.switch(part, branches, payload)
    return payload


def correlate_kernel(
    own_ref, far_ref, inverse_ref, own_mask_ref, far_mask_ref, out_ref, planes, cross, *, rows, chunk, band
):
    far_stations = planes.shape[1]

    @pl.when(pl.program_id(1) == 0)
    def _():
        planes[...] = far_ref[0].astype(jnp.float32)

    def one(i, carry):
        own = own_ref[i].astype(jnp.float32)
        for start in range(0, far_stations, chunk):
            cut = pl.ds(start, chunk)
            acc_re = jnp.zeros((chunk, H), jnp.float32)
            acc_im = jnp.zeros((chunk, H), jnp.float32)
            for g in range(4):
                a_re = own[g : g + 1, :]
                a_im = own[4 + g : 5 + g, :]
                b_re = planes[g, cut, :]
                b_im = planes[4 + g, cut, :]
                acc_re = acc_re + a_re * b_re + a_im * b_im
                acc_im = acc_im + a_re * b_im - a_im * b_re
            place = pl.ds(pl.multiple_of(i * far_stations + start, chunk), chunk)
            cross[place, 0:H] = acc_re.astype(cross.dtype)
            cross[place, H:SEG] = acc_im.astype(cross.dtype)
        return carry

    lax.fori_loop(0, rows, one, 0)
    own_mask = own_mask_ref[0]
    far_mask = far_mask_ref[0]
    counts = far_mask[:, 0:1] * own_mask[0:1, :]
    for g in range(1, own_mask.shape[0]):
        counts = counts + far_mask[:, g : g + 1] * own_mask[g : g + 1, :]
    scale = 1.0 / (math.sqrt(SEG) * jnp.maximum(counts, 1.0))
    for first in range(0, rows * far_stations, band):
        summed = jnp.dot(
            cross[first : first + band, :], inverse_ref[...], preferred_element_type=jnp.float32
        )
        for piece in range(band // far_stations):
            i = first // far_stations + piece
            rows_of = summed[piece * far_stations : (piece + 1) * far_stations, :]
            out_ref[0, i] = (rows_of * scale[:, i : i + 1]).astype(out_ref.dtype)


def correlate(own_parts, far_planes, inverse, own_mask, far_masks, rows=16, chunk=32, band=256):
    stations = own_parts.shape[0]
    rounds, parts, far_stations, bins = far_planes.shape
    segments = own_mask.shape[1]
    own_mask = own_mask.astype(jnp.float32).reshape(stations // rows, rows, segments).transpose(0, 2, 1)
    return pl.pallas_call(
        functools.partial(correlate_kernel, rows=rows, chunk=chunk, band=band),
        grid=(rounds, stations // rows),
        in_specs=[
            pl.BlockSpec((rows, parts, bins), lambda r, b: (b, 0, 0)),
            pl.BlockSpec((1, parts, far_stations, bins), lambda r, b: (r, 0, 0, 0)),
            pl.BlockSpec((SEG, SEG), lambda r, b: (0, 0)),
            pl.BlockSpec((1, segments, rows), lambda r, b: (b, 0, 0)),
            pl.BlockSpec((1, far_stations, segments), lambda r, b: (r, 0, 0)),
        ],
        out_specs=pl.BlockSpec((1, rows, far_stations, SEG), lambda r, b: (r, b, 0, 0)),
        out_shape=jax.ShapeDtypeStruct((rounds, stations, far_stations, SEG), jnp.bfloat16),
        scratch_shapes=[
            pltpu.VMEM((parts, far_stations, bins), jnp.float32),
            pltpu.VMEM((rows * far_stations, SEG), jnp.bfloat16),
        ],
        compiler_params=pltpu.CompilerParams(dimension_semantics=("arbitrary", "arbitrary")),
    )(own_parts, far_planes, inverse, own_mask, far_masks.astype(jnp.float32))


def shards(records, record_station, taps, gap_mask, partners):
    per_block = taps.shape[0]
    block_total = lax.axis_size("dev")
    my_index = lax.axis_index("dev")
    ordered = place_records(records, record_station, per_block, block_total, my_index)
    own_spec = whiten(ordered, taps, gap_mask)
    mask_row = jnp.zeros((1, SEG), jnp.bfloat16).at[0, : per_block * NSEG].set(
        gap_mask.reshape(-1).astype(jnp.bfloat16)
    )
    payload = jnp.concatenate([own_spec.reshape(per_block * NSEG, SEG), mask_row], axis=0)
    half = per_block * NSEG // 2
    pieces = (payload[:half], payload[half:])
    rounds = partners.shape[0]
    codes = jnp.bitwise_xor(my_index, partners[:, my_index])

    def fetch(round_index, gathered):
        arrived = exchange(pieces, codes[round_index], block_total)
        return tuple(
            lax.dynamic_update_index_in_dim(kept, piece, round_index, 0)
            for kept, piece in zip(gathered, arrived)
        )

    gathered = lax.fori_loop(
        0,
        rounds,
        fetch,
        tuple(jnp.zeros((rounds,) + piece.shape, piece.dtype) for piece in pieces),
    )
    gathered = jnp.concatenate(gathered, axis=1)
    far = gathered[:, : per_block * NSEG].reshape(rounds, per_block, NSEG, SEG)
    far_masks = gathered[:, per_block * NSEG, : per_block * NSEG].reshape(rounds, per_block, NSEG)
    own_parts = jnp.concatenate([own_spec[..., :H], own_spec[..., H:]], axis=1)
    far_planes = jnp.concatenate([far[..., :H], far[..., H:]], axis=2).transpose(0, 2, 1, 3)
    return correlate(own_parts, far_planes, inverse_table(), gap_mask, far_masks)


def solution(mesh):
    in_specs = (P("dev", None), P("dev"), P("dev", None), P("dev", None), P())
    out_specs = P(None, "dev", None, None)
    return jax.shard_map(shards, mesh=mesh, in_specs=in_specs, out_specs=out_specs, check_vma=False)
```

```python
import functools
import math

import jax
import jax.numpy as jnp
from jax import lax
from jax.experimental import pallas as pl
from jax.experimental.pallas import tpu as pltpu
from jax.sharding import PartitionSpec as P

SEG = 512
H = SEG // 2
TAPS = 255
NSEG = 4


def angle_table(row_count, col_count):
    first = jnp.arange(row_count, dtype=jnp.int32)[:, None]
    second = jnp.arange(col_count, dtype=jnp.int32)[None, :]
    return 2.0 * math.pi / SEG * (first * second % SEG).astype(jnp.float32)


def forward_table(row_count):
    phase = angle_table(row_count, SEG // 2)
    return jnp.concatenate([jnp.cos(phase), -jnp.sin(phase)], axis=1).astype(jnp.bfloat16)


def inverse_table():
    phase = angle_table(SEG // 2, SEG)
    weights = jnp.where(jnp.arange(SEG // 2, dtype=jnp.int32) == 0, 1.0, 2.0).astype(jnp.float32)[
        :, None
    ]
    return jnp.concatenate([weights * jnp.cos(phase), -weights * jnp.sin(phase)], axis=0).astype(
        jnp.bfloat16
    )


def whiten(ordered, taps, gap_mask):
    station_count = ordered.shape[0]
    pieces = ordered.reshape(station_count, NSEG, SEG).astype(jnp.float32)
    scaled = pieces * lax.rsqrt(jnp.mean(pieces * pieces, axis=2, keepdims=True) + 1e-06)
    normed = scaled.astype(jnp.bfloat16)
    spectrum = jnp.dot(
        normed.reshape(station_count * NSEG, SEG),
        forward_table(SEG),
        preferred_element_type=jnp.float32,
    )
    spectrum = spectrum.reshape(station_count, NSEG, SEG)
    response = jnp.dot(taps, forward_table(TAPS), preferred_element_type=jnp.float32)[:, None, :]
    half_bins = SEG // 2
    spec_re = spectrum[:, :, :half_bins]
    spec_im = spectrum[:, :, half_bins:]
    resp_re = response[:, :, :half_bins]
    resp_im = response[:, :, half_bins:]
    weight = gap_mask.astype(jnp.float32)[:, :, None]
    white_re = (spec_re * resp_re - spec_im * resp_im) * weight
    white_im = (spec_re * resp_im + spec_im * resp_re) * weight
    return jnp.concatenate([white_re, white_im], axis=2).astype(jnp.bfloat16)


def place_records(records, record_station, per_block, block_total, my_index):
    owners = record_station // per_block
    label = (record_station - owners * per_block + 1).astype(records.dtype)
    tagged = jnp.concatenate(
        [records, jnp.broadcast_to(label[:, None], (records.shape[0], 128))], axis=1
    )
    outgoing = jnp.zeros((block_total, tagged.shape[1]), records.dtype).at[owners].set(tagged)
    arrived = lax.all_to_all(outgoing, "dev", split_axis=0, concat_axis=0, tiled=True)
    local_rows = arrived[:, records.shape[1]].astype(jnp.int32) - 1
    local_rows = jnp.where(local_rows >= 0, local_rows, per_block)
    return (
        jnp.zeros((per_block, records.shape[1]), records.dtype)
        .at[local_rows]
        .set(arrived[:, : records.shape[1]], mode="drop")
    )


def exchange(payload, code, device_total, cover=None):
    levels = device_total.bit_length() - 1
    groups = [(0, min(3, levels))]
    if levels > 3:
        groups.append((3, levels - 3))

    def send(mask, value):
        pairs = [(source, source ^ mask) for source in range(device_total)]
        return lax.ppermute(value, "dev", pairs)

    covered = None
    for stage, (shift, width) in enumerate(groups):
        part = jnp.bitwise_and(jnp.right_shift(code, shift), 2**width - 1)
        moves = [lambda value: value] + [
            functools.partial(send, step << shift) for step in range(1, 2**width)
        ]
        if stage == 0 and cover is not None:
            work, inputs = cover

            def with_cover(move, operands):
                value, extra = operands
                return move(value), work(*extra)

            branches = [functools.partial(with_cover, move) for move in moves]
            payload, covered = lax.switch(part, branches, (payload, inputs))
        else:
            payload = lax.switch(part, moves, payload)
    return payload, covered


def correlate_kernel(
    own_ref, far_ref, inverse_ref, own_mask_ref, far_mask_ref, out_ref, planes, cross, *, rows, chunk, band
):
    far_stations = planes.shape[1]

    @pl.when(pl.program_id(1) == 0)
    def _():
        planes[...] = far_ref[0].astype(jnp.float32)

    def one(i, carry):
        own = own_ref[i].astype(jnp.float32)
        for start in range(0, far_stations, chunk):
            cut = pl.ds(start, chunk)
            acc_re = jnp.zeros((chunk, H), jnp.float32)
            acc_im = jnp.zeros((chunk, H), jnp.float32)
            for g in range(4):
                a_re = own[g : g + 1, :]
                a_im = own[4 + g : 5 + g, :]
                b_re = planes[g, cut, :]
                b_im = planes[4 + g, cut, :]
                acc_re = acc_re + a_re * b_re + a_im * b_im
                acc_im = acc_im + a_re * b_im - a_im * b_re
            place = pl.ds(pl.multiple_of(i * far_stations + start, chunk), chunk)
            cross[place, 0:H] = acc_re.astype(cross.dtype)
            cross[place, H:SEG] = acc_im.astype(cross.dtype)
        return carry

    lax.fori_loop(0, rows, one, 0)
    own_mask = own_mask_ref[0]
    far_mask = far_mask_ref[0]
    counts = far_mask[:, 0:1] * own_mask[0:1, :]
    for g in range(1, own_mask.shape[0]):
        counts = counts + far_mask[:, g : g + 1] * own_mask[g : g + 1, :]
    scale = 1.0 / (math.sqrt(SEG) * jnp.maximum(counts, 1.0))
    for first in range(0, rows * far_stations, band):
        summed = jnp.dot(
            cross[first : first + band, :], inverse_ref[...], preferred_element_type=jnp.float32
        )
        for piece in range(band // far_stations):
            i = first // far_stations + piece
            rows_of = summed[piece * far_stations : (piece + 1) * far_stations, :]
            out_ref[0, i] = (rows_of * scale[:, i : i + 1]).astype(out_ref.dtype)


def correlate(own_parts, far_planes, inverse, own_mask, far_masks, rows=16, chunk=32, band=256):
    stations = own_parts.shape[0]
    rounds, parts, far_stations, bins = far_planes.shape
    segments = own_mask.shape[1]
    own_mask = own_mask.astype(jnp.float32).reshape(stations // rows, rows, segments).transpose(0, 2, 1)
    return pl.pallas_call(
        functools.partial(correlate_kernel, rows=rows, chunk=chunk, band=band),
        grid=(rounds, stations // rows),
        in_specs=[
            pl.BlockSpec((rows, parts, bins), lambda r, b: (b, 0, 0)),
            pl.BlockSpec((1, parts, far_stations, bins), lambda r, b: (r, 0, 0, 0)),
            pl.BlockSpec((SEG, SEG), lambda r, b: (0, 0)),
            pl.BlockSpec((1, segments, rows), lambda r, b: (b, 0, 0)),
            pl.BlockSpec((1, far_stations, segments), lambda r, b: (r, 0, 0)),
        ],
        out_specs=pl.BlockSpec((1, rows, far_stations, SEG), lambda r, b: (r, b, 0, 0)),
        out_shape=jax.ShapeDtypeStruct((rounds, stations, far_stations, SEG), jnp.bfloat16),
        scratch_shapes=[
            pltpu.VMEM((parts, far_stations, bins), jnp.float32),
            pltpu.VMEM((rows * far_stations, SEG), jnp.bfloat16),
        ],
        compiler_params=pltpu.CompilerParams(dimension_semantics=("arbitrary", "arbitrary")),
    )(own_parts, far_planes, inverse, own_mask, far_masks.astype(jnp.float32))


def shards(records, record_station, taps, gap_mask, partners):
    per_block = taps.shape[0]
    block_total = lax.axis_size("dev")
    my_index = lax.axis_index("dev")
    ordered = place_records(records, record_station, per_block, block_total, my_index)
    own_spec = whiten(ordered, taps, gap_mask)
    mask_row = jnp.zeros((1, SEG), jnp.bfloat16).at[0, : per_block * NSEG].set(
        gap_mask.reshape(-1).astype(jnp.bfloat16)
    )
    payload = jnp.concatenate([own_spec.reshape(per_block * NSEG, SEG), mask_row], axis=0)
    half = per_block * NSEG // 2
    pieces = (payload[:half], payload[half:])
    rounds = partners.shape[0]
    codes = jnp.bitwise_xor(my_index, partners[:, my_index])

    own_parts = jnp.concatenate([own_spec[..., :H], own_spec[..., H:]], axis=1)
    inverse = inverse_table()
    rows = per_block * NSEG

    def planes_of(joined):
        far = joined[:rows].reshape(1, per_block, NSEG, SEG)
        far_mask = joined[rows, :rows].reshape(1, per_block, NSEG)
        return jnp.concatenate([far[..., :H], far[..., H:]], axis=2).transpose(0, 2, 1, 3), far_mask

    def work(first, second):
        far_planes, far_mask = planes_of(jnp.concatenate([first, second], axis=0))
        return correlate(own_parts, far_planes, inverse, gap_mask, far_mask)

    def fetch(round_index, carry):
        gathered, result = carry
        earlier = jnp.maximum(round_index - 1, 0)
        inputs = (gathered[0][earlier], gathered[1][earlier])
        arrived, done = exchange(pieces, codes[round_index], block_total, (work, inputs))
        gathered = tuple(
            lax.dynamic_update_index_in_dim(kept, piece, round_index, 0)
            for kept, piece in zip(gathered, arrived)
        )
        result = lax.dynamic_update_slice_in_dim(result, done, earlier, 0)
        return gathered, result

    gathered, result = lax.fori_loop(
        0,
        rounds,
        fetch,
        (
            tuple(jnp.zeros((rounds,) + piece.shape, piece.dtype) for piece in pieces),
            jnp.zeros((rounds, per_block, per_block, SEG), jnp.bfloat16),
        ),
    )
    last = work(gathered[0][rounds - 1], gathered[1][rounds - 1])
    return lax.dynamic_update_slice_in_dim(result, last, rounds - 1, 0)


def solution(mesh):
    in_specs = (P("dev", None), P("dev"), P("dev", None), P("dev", None), P())
    out_specs = P(None, "dev", None, None)
    return jax.shard_map(shards, mesh=mesh, in_specs=in_specs, out_specs=out_specs, check_vma=False)
```

```python
import functools
import math

import jax
import jax.numpy as jnp
from jax import lax
from jax.experimental import pallas as pl
from jax.experimental.pallas import tpu as pltpu
from jax.sharding import PartitionSpec as P

SEG = 512
H = SEG // 2
TAPS = 255
NSEG = 4


def angle_table(row_count, col_count):
    first = jnp.arange(row_count, dtype=jnp.int32)[:, None]
    second = jnp.arange(col_count, dtype=jnp.int32)[None, :]
    return 2.0 * math.pi / SEG * (first * second % SEG).astype(jnp.float32)


def forward_table(row_count):
    phase = angle_table(row_count, SEG // 2)
    return jnp.concatenate([jnp.cos(phase), -jnp.sin(phase)], axis=1).astype(jnp.bfloat16)


def inverse_table():
    phase = angle_table(SEG // 2, SEG)
    weights = jnp.where(jnp.arange(SEG // 2, dtype=jnp.int32) == 0, 1.0, 2.0).astype(jnp.float32)[
        :, None
    ]
    return jnp.concatenate([weights * jnp.cos(phase), -weights * jnp.sin(phase)], axis=0).astype(
        jnp.bfloat16
    )


def whiten(ordered, taps, gap_mask):
    station_count = ordered.shape[0]
    pieces = ordered.reshape(station_count, NSEG, SEG).astype(jnp.float32)
    scaled = pieces * lax.rsqrt(jnp.mean(pieces * pieces, axis=2, keepdims=True) + 1e-06)
    normed = scaled.astype(jnp.bfloat16)
    spectrum = jnp.dot(
        normed.reshape(station_count * NSEG, SEG),
        forward_table(SEG),
        preferred_element_type=jnp.float32,
    )
    spectrum = spectrum.reshape(station_count, NSEG, SEG)
    response = jnp.dot(taps, forward_table(TAPS), preferred_element_type=jnp.float32)[:, None, :]
    half_bins = SEG // 2
    spec_re = spectrum[:, :, :half_bins]
    spec_im = spectrum[:, :, half_bins:]
    resp_re = response[:, :, :half_bins]
    resp_im = response[:, :, half_bins:]
    weight = gap_mask.astype(jnp.float32)[:, :, None]
    white_re = (spec_re * resp_re - spec_im * resp_im) * weight
    white_im = (spec_re * resp_im + spec_im * resp_re) * weight
    return jnp.concatenate([white_re, white_im], axis=2).astype(jnp.bfloat16)


def place_records(records, record_station, per_block, block_total, my_index):
    owners = record_station // per_block
    label = (record_station - owners * per_block + 1).astype(records.dtype)
    tagged = jnp.concatenate(
        [records, jnp.broadcast_to(label[:, None], (records.shape[0], 128))], axis=1
    )
    outgoing = jnp.zeros((block_total, tagged.shape[1]), records.dtype).at[owners].set(tagged)
    arrived = lax.all_to_all(outgoing, "dev", split_axis=0, concat_axis=0, tiled=True)
    local_rows = arrived[:, records.shape[1]].astype(jnp.int32) - 1
    local_rows = jnp.where(local_rows >= 0, local_rows, per_block)
    return (
        jnp.zeros((per_block, records.shape[1]), records.dtype)
        .at[local_rows]
        .set(arrived[:, : records.shape[1]], mode="drop")
    )


def exchange(payload, code, device_total):
    levels = device_total.bit_length() - 1
    groups = [(0, min(3, levels))]
    if levels > 3:
        groups.append((3, levels - 3))

    def send(mask, value):
        pairs = [(source, source ^ mask) for source in range(device_total)]
        return lax.ppermute(value, "dev", pairs)

    for shift, width in groups:
        part = jnp.bitwise_and(jnp.right_shift(code, shift), 2**width - 1)
        branches = [lambda value: value] + [
            functools.partial(send, step << shift) for step in range(1, 2**width)
        ]
        payload = lax.switch(part, branches, payload)
    return payload


def correlate_kernel(
    own_ref, far_ref, inverse_ref, own_mask_ref, far_mask_ref, out_ref, planes, cross, *, rows, chunk, band
):
    far_stations = planes.shape[1]

    @pl.when(pl.program_id(1) == 0)
    def _():
        planes[...] = far_ref[0].astype(jnp.float32)

    def one(i, carry):
        own = own_ref[i].astype(jnp.float32)
        for start in range(0, far_stations, chunk):
            cut = pl.ds(start, chunk)
            acc_re = jnp.zeros((chunk, H), jnp.float32)
            acc_im = jnp.zeros((chunk, H), jnp.float32)
            for g in range(4):
                a_re = own[g : g + 1, :]
                a_im = own[4 + g : 5 + g, :]
                b_re = planes[g, cut, :]
                b_im = planes[4 + g, cut, :]
                acc_re = acc_re + a_re * b_re + a_im * b_im
                acc_im = acc_im + a_re * b_im - a_im * b_re
            place = pl.ds(pl.multiple_of(i * far_stations + start, chunk), chunk)
            cross[place, 0:H] = acc_re.astype(cross.dtype)
            cross[place, H:SEG] = acc_im.astype(cross.dtype)
        return carry

    lax.fori_loop(0, rows, one, 0)
    own_mask = own_mask_ref[0]
    far_mask = far_mask_ref[0]
    counts = far_mask[:, 0:1] * own_mask[0:1, :]
    for g in range(1, own_mask.shape[0]):
        counts = counts + far_mask[:, g : g + 1] * own_mask[g : g + 1, :]
    scale = 1.0 / (math.sqrt(SEG) * jnp.maximum(counts, 1.0))
    for first in range(0, rows * far_stations, band):
        summed = jnp.dot(
            cross[first : first + band, :], inverse_ref[...], preferred_element_type=jnp.float32
        )
        for piece in range(band // far_stations):
            i = first // far_stations + piece
            rows_of = summed[piece * far_stations : (piece + 1) * far_stations, :]
            out_ref[0, i] = (rows_of * scale[:, i : i + 1]).astype(out_ref.dtype)


def correlate(own_parts, far_planes, inverse, own_mask, far_masks, rows=16, chunk=32, band=256):
    stations = own_parts.shape[0]
    rounds, parts, far_stations, bins = far_planes.shape
    segments = own_mask.shape[1]
    own_mask = own_mask.astype(jnp.float32).reshape(stations // rows, rows, segments).transpose(0, 2, 1)
    return pl.pallas_call(
        functools.partial(correlate_kernel, rows=rows, chunk=chunk, band=band),
        grid=(rounds, stations // rows),
        in_specs=[
            pl.BlockSpec((rows, parts, bins), lambda r, b: (b, 0, 0)),
            pl.BlockSpec((1, parts, far_stations, bins), lambda r, b: (r, 0, 0, 0)),
            pl.BlockSpec((SEG, SEG), lambda r, b: (0, 0)),
            pl.BlockSpec((1, segments, rows), lambda r, b: (b, 0, 0)),
            pl.BlockSpec((1, far_stations, segments), lambda r, b: (r, 0, 0)),
        ],
        out_specs=pl.BlockSpec((1, rows, far_stations, SEG), lambda r, b: (r, b, 0, 0)),
        out_shape=jax.ShapeDtypeStruct((rounds, stations, far_stations, SEG), jnp.bfloat16),
        scratch_shapes=[
            pltpu.VMEM((parts, far_stations, bins), jnp.float32),
            pltpu.VMEM((rows * far_stations, SEG), jnp.bfloat16),
        ],
        compiler_params=pltpu.CompilerParams(dimension_semantics=("arbitrary", "arbitrary")),
    )(own_parts, far_planes, inverse, own_mask, far_masks.astype(jnp.float32))


def shards(records, record_station, taps, gap_mask, partners):
    per_block = taps.shape[0]
    block_total = lax.axis_size("dev")
    my_index = lax.axis_index("dev")
    ordered = place_records(records, record_station, per_block, block_total, my_index)
    own_spec = whiten(ordered, taps, gap_mask)
    mask_row = jnp.zeros((1, SEG), jnp.bfloat16).at[0, : per_block * NSEG].set(
        gap_mask.reshape(-1).astype(jnp.bfloat16)
    )
    payload = jnp.concatenate([own_spec.reshape(per_block * NSEG, SEG), mask_row], axis=0)
    rounds = partners.shape[0]
    codes = jnp.bitwise_xor(my_index, partners[:, my_index])

    def fetch(round_index, gathered):
        arrived = exchange(payload, codes[round_index], block_total)
        return lax.dynamic_update_index_in_dim(gathered, arrived, round_index, 0)

    gathered = lax.fori_loop(
        0, rounds, fetch, jnp.zeros((rounds,) + payload.shape, payload.dtype)
    )
    far = gathered[:, : per_block * NSEG].reshape(rounds, per_block, NSEG, SEG)
    far_masks = gathered[:, per_block * NSEG, : per_block * NSEG].reshape(rounds, per_block, NSEG)
    own_parts = jnp.concatenate([own_spec[..., :H], own_spec[..., H:]], axis=1)
    far_planes = jnp.concatenate([far[..., :H], far[..., H:]], axis=2).transpose(0, 2, 1, 3)
    return correlate(own_parts, far_planes, inverse_table(), gap_mask, far_masks)


def solution(mesh):
    in_specs = (P("dev", None), P("dev"), P("dev", None), P("dev", None), P())
    out_specs = P(None, "dev", None, None)
    return jax.shard_map(shards, mesh=mesh, in_specs=in_specs, out_specs=out_specs, check_vma=False)
```

```python
import functools
import math

import jax
import jax.numpy as jnp
from jax import lax
from jax.experimental import pallas as pl
from jax.experimental.pallas import tpu as pltpu
from jax.sharding import PartitionSpec as P

SEG = 512
H = SEG // 2
TAPS = 255
NSEG = 4


def angle_table(row_count, col_count):
    first = jnp.arange(row_count, dtype=jnp.int32)[:, None]
    second = jnp.arange(col_count, dtype=jnp.int32)[None, :]
    return 2.0 * math.pi / SEG * (first * second % SEG).astype(jnp.float32)


def forward_table(row_count):
    phase = angle_table(row_count, SEG // 2)
    return jnp.concatenate([jnp.cos(phase), -jnp.sin(phase)], axis=1).astype(jnp.bfloat16)


def inverse_table():
    phase = angle_table(SEG // 2, SEG)
    weights = jnp.where(jnp.arange(SEG // 2, dtype=jnp.int32) == 0, 1.0, 2.0).astype(jnp.float32)[
        :, None
    ]
    return jnp.concatenate([weights * jnp.cos(phase), -weights * jnp.sin(phase)], axis=0).astype(
        jnp.bfloat16
    )


def whiten(ordered, taps, gap_mask):
    station_count = ordered.shape[0]
    pieces = ordered.reshape(station_count, NSEG, SEG).astype(jnp.float32)
    scaled = pieces * lax.rsqrt(jnp.mean(pieces * pieces, axis=2, keepdims=True) + 1e-06)
    normed = scaled.astype(jnp.bfloat16)
    spectrum = jnp.dot(
        normed.reshape(station_count * NSEG, SEG),
        forward_table(SEG),
        preferred_element_type=jnp.float32,
    )
    spectrum = spectrum.reshape(station_count, NSEG, SEG)
    response = jnp.dot(taps, forward_table(TAPS), preferred_element_type=jnp.float32)[:, None, :]
    half_bins = SEG // 2
    spec_re = spectrum[:, :, :half_bins]
    spec_im = spectrum[:, :, half_bins:]
    resp_re = response[:, :, :half_bins]
    resp_im = response[:, :, half_bins:]
    weight = gap_mask.astype(jnp.float32)[:, :, None]
    white_re = (spec_re * resp_re - spec_im * resp_im) * weight
    white_im = (spec_re * resp_im + spec_im * resp_re) * weight
    return jnp.concatenate([white_re, white_im], axis=2).astype(jnp.bfloat16)


def place_records(records, record_station, per_block, block_total, my_index):
    owners = record_station // per_block
    label = (record_station - owners * per_block + 1).astype(records.dtype)
    tagged = jnp.concatenate(
        [records, jnp.broadcast_to(label[:, None], (records.shape[0], 128))], axis=1
    )
    slots = jnp.arange(block_total, dtype=jnp.int32)
    sending = (slots[:, None] == owners[None, :]).astype(records.dtype)
    outgoing = jnp.dot(sending, tagged, preferred_element_type=jnp.float32).astype(records.dtype)
    arrived = lax.all_to_all(outgoing, "dev", split_axis=0, concat_axis=0, tiled=True)
    local_rows = arrived[:, records.shape[1]].astype(jnp.int32) - 1
    places = jnp.arange(per_block, dtype=jnp.int32)
    taking = (places[:, None] == local_rows[None, :]).astype(records.dtype)
    return jnp.dot(
        taking, arrived[:, : records.shape[1]], preferred_element_type=jnp.float32
    ).astype(records.dtype)


def exchange(payload, code, device_total):
    levels = device_total.bit_length() - 1
    groups = [(0, min(3, levels))]
    if levels > 3:
        groups.append((3, levels - 3))

    def send(mask, value):
        pairs = [(source, source ^ mask) for source in range(device_total)]
        return lax.ppermute(value, "dev", pairs)

    for shift, width in groups:
        part = jnp.bitwise_and(jnp.right_shift(code, shift), 2**width - 1)
        branches = [lambda value: value] + [
            functools.partial(send, step << shift) for step in range(1, 2**width)
        ]
        payload = lax.switch(part, branches, payload)
    return payload


def correlate_kernel(
    own_ref, far_ref, inverse_ref, own_mask_ref, far_mask_ref, out_ref, planes, cross, *, rows, chunk, band
):
    far_stations = planes.shape[1]

    @pl.when(pl.program_id(1) == 0)
    def _():
        planes[...] = far_ref[0].astype(jnp.float32)

    def one(i, carry):
        own = own_ref[i].astype(jnp.float32)
        for start in range(0, far_stations, chunk):
            cut = pl.ds(start, chunk)
            acc_re = jnp.zeros((chunk, H), jnp.float32)
            acc_im = jnp.zeros((chunk, H), jnp.float32)
            for g in range(4):
                a_re = own[g : g + 1, :]
                a_im = own[4 + g : 5 + g, :]
                b_re = planes[g, cut, :]
                b_im = planes[4 + g, cut, :]
                acc_re = acc_re + a_re * b_re + a_im * b_im
                acc_im = acc_im + a_re * b_im - a_im * b_re
            place = pl.ds(pl.multiple_of(i * far_stations + start, chunk), chunk)
            cross[place, 0:H] = acc_re.astype(cross.dtype)
            cross[place, H:SEG] = acc_im.astype(cross.dtype)
        return carry

    lax.fori_loop(0, rows, one, 0)
    own_mask = own_mask_ref[0]
    far_mask = far_mask_ref[0]
    counts = far_mask[:, 0:1] * own_mask[0:1, :]
    for g in range(1, own_mask.shape[0]):
        counts = counts + far_mask[:, g : g + 1] * own_mask[g : g + 1, :]
    scale = 1.0 / (math.sqrt(SEG) * jnp.maximum(counts, 1.0))
    for first in range(0, rows * far_stations, band):
        summed = jnp.dot(
            cross[first : first + band, :], inverse_ref[...], preferred_element_type=jnp.float32
        )
        for piece in range(band // far_stations):
            i = first // far_stations + piece
            rows_of = summed[piece * far_stations : (piece + 1) * far_stations, :]
            out_ref[0, i] = (rows_of * scale[:, i : i + 1]).astype(out_ref.dtype)


def correlate(own_parts, far_planes, inverse, own_mask, far_masks, rows=16, chunk=32, band=256):
    stations = own_parts.shape[0]
    rounds, parts, far_stations, bins = far_planes.shape
    segments = own_mask.shape[1]
    own_mask = own_mask.astype(jnp.float32).reshape(stations // rows, rows, segments).transpose(0, 2, 1)
    return pl.pallas_call(
        functools.partial(correlate_kernel, rows=rows, chunk=chunk, band=band),
        grid=(rounds, stations // rows),
        in_specs=[
            pl.BlockSpec((rows, parts, bins), lambda r, b: (b, 0, 0)),
            pl.BlockSpec((1, parts, far_stations, bins), lambda r, b: (r, 0, 0, 0)),
            pl.BlockSpec((SEG, SEG), lambda r, b: (0, 0)),
            pl.BlockSpec((1, segments, rows), lambda r, b: (b, 0, 0)),
            pl.BlockSpec((1, far_stations, segments), lambda r, b: (r, 0, 0)),
        ],
        out_specs=pl.BlockSpec((1, rows, far_stations, SEG), lambda r, b: (r, b, 0, 0)),
        out_shape=jax.ShapeDtypeStruct((rounds, stations, far_stations, SEG), jnp.bfloat16),
        scratch_shapes=[
            pltpu.VMEM((parts, far_stations, bins), jnp.float32),
            pltpu.VMEM((rows * far_stations, SEG), jnp.bfloat16),
        ],
        compiler_params=pltpu.CompilerParams(dimension_semantics=("arbitrary", "arbitrary")),
    )(own_parts, far_planes, inverse, own_mask, far_masks.astype(jnp.float32))


def shards(records, record_station, taps, gap_mask, partners):
    per_block = taps.shape[0]
    block_total = lax.axis_size("dev")
    my_index = lax.axis_index("dev")
    ordered = place_records(records, record_station, per_block, block_total, my_index)
    own_spec = whiten(ordered, taps, gap_mask)
    mask_row = jnp.zeros((1, SEG), jnp.bfloat16).at[0, : per_block * NSEG].set(
        gap_mask.reshape(-1).astype(jnp.bfloat16)
    )
    payload = jnp.concatenate([own_spec.reshape(per_block * NSEG, SEG), mask_row], axis=0)
    rounds = partners.shape[0]
    codes = jnp.bitwise_xor(my_index, partners[:, my_index])

    def fetch(round_index, gathered):
        arrived = exchange(payload, codes[round_index], block_total)
        return lax.dynamic_update_index_in_dim(gathered, arrived, round_index, 0)

    gathered = lax.fori_loop(
        0, rounds, fetch, jnp.zeros((rounds,) + payload.shape, payload.dtype)
    )
    far = gathered[:, : per_block * NSEG].reshape(rounds, per_block, NSEG, SEG)
    far_masks = gathered[:, per_block * NSEG, : per_block * NSEG].reshape(rounds, per_block, NSEG)
    own_parts = jnp.concatenate([own_spec[..., :H], own_spec[..., H:]], axis=1)
    far_planes = jnp.concatenate([far[..., :H], far[..., H:]], axis=2).transpose(0, 2, 1, 3)
    return correlate(own_parts, far_planes, inverse_table(), gap_mask, far_masks)


def solution(mesh):
    in_specs = (P("dev", None), P("dev"), P("dev", None), P("dev", None), P())
    out_specs = P(None, "dev", None, None)
    return jax.shard_map(shards, mesh=mesh, in_specs=in_specs, out_specs=out_specs, check_vma=False)
```

```python
import functools
import math

import jax
import jax.numpy as jnp
from jax import lax
from jax.experimental import pallas as pl
from jax.experimental.pallas import tpu as pltpu
from jax.sharding import PartitionSpec as P

SEG = 512
H = SEG // 2
TAPS = 255
NSEG = 4


def angle_table(row_count, col_count):
    first = jnp.arange(row_count, dtype=jnp.int32)[:, None]
    second = jnp.arange(col_count, dtype=jnp.int32)[None, :]
    return 2.0 * math.pi / SEG * (first * second % SEG).astype(jnp.float32)


def forward_table(row_count):
    phase = angle_table(row_count, SEG // 2)
    return jnp.concatenate([jnp.cos(phase), -jnp.sin(phase)], axis=1).astype(jnp.bfloat16)


def inverse_table():
    phase = angle_table(SEG // 2, SEG)
    weights = jnp.where(jnp.arange(SEG // 2, dtype=jnp.int32) == 0, 1.0, 2.0).astype(jnp.float32)[
        :, None
    ]
    return jnp.concatenate([weights * jnp.cos(phase), -weights * jnp.sin(phase)], axis=0).astype(
        jnp.bfloat16
    )


def whiten(ordered, taps, gap_mask):
    station_count = ordered.shape[0]
    pieces = ordered.reshape(station_count, NSEG, SEG).astype(jnp.float32)
    scaled = pieces * lax.rsqrt(jnp.mean(pieces * pieces, axis=2, keepdims=True) + 1e-06)
    normed = scaled.astype(jnp.bfloat16)
    spectrum = jnp.dot(
        normed.reshape(station_count * NSEG, SEG),
        forward_table(SEG),
        preferred_element_type=jnp.float32,
    )
    spectrum = spectrum.reshape(station_count, NSEG, SEG)
    response = jnp.dot(taps, forward_table(TAPS), preferred_element_type=jnp.float32)[:, None, :]
    half_bins = SEG // 2
    spec_re = spectrum[:, :, :half_bins]
    spec_im = spectrum[:, :, half_bins:]
    resp_re = response[:, :, :half_bins]
    resp_im = response[:, :, half_bins:]
    weight = gap_mask.astype(jnp.float32)[:, :, None]
    white_re = (spec_re * resp_re - spec_im * resp_im) * weight
    white_im = (spec_re * resp_im + spec_im * resp_re) * weight
    return jnp.concatenate([white_re, white_im], axis=2).astype(jnp.bfloat16)


def place_records(records, record_station, per_block, block_total, my_index):
    owners = record_station // per_block
    label = (record_station - owners * per_block + 1).astype(records.dtype)
    tagged = jnp.concatenate(
        [records, jnp.broadcast_to(label[:, None], (records.shape[0], 128))], axis=1
    )
    slots = jnp.arange(block_total, dtype=jnp.int32)
    sending = (slots[:, None] == owners[None, :]).astype(records.dtype)
    outgoing = jnp.dot(sending, tagged, preferred_element_type=jnp.float32).astype(records.dtype)
    arrived = lax.all_to_all(outgoing, "dev", split_axis=0, concat_axis=0, tiled=True)
    local_rows = arrived[:, records.shape[1]].astype(jnp.int32) - 1
    places = jnp.arange(per_block, dtype=jnp.int32)
    taking = (places[:, None] == local_rows[None, :]).astype(records.dtype)
    return jnp.dot(
        taking, arrived[:, : records.shape[1]], preferred_element_type=jnp.float32
    ).astype(records.dtype)


def exchange(payload, code, device_total):
    levels = device_total.bit_length() - 1
    groups = [(0, min(3, levels))]
    if levels > 3:
        groups.append((3, levels - 3))

    def send(mask, value):
        pairs = [(source, source ^ mask) for source in range(device_total)]
        return lax.ppermute(value, "dev", pairs)

    for shift, width in groups:
        part = jnp.bitwise_and(jnp.right_shift(code, shift), 2**width - 1)
        branches = [lambda value: value] + [
            functools.partial(send, step << shift) for step in range(1, 2**width)
        ]
        payload = lax.switch(part, branches, payload)
    return payload


def correlate_kernel(
    own_ref, far_ref, inverse_ref, own_mask_ref, far_mask_ref, out_ref, planes, cross, *, rows, chunk, band
):
    far_stations = planes.shape[1]

    @pl.when(pl.program_id(1) == 0)
    def _():
        planes[...] = far_ref[0].astype(jnp.float32)

    def one(i, carry):
        own = own_ref[i].astype(jnp.float32)
        for start in range(0, far_stations, chunk):
            cut = pl.ds(start, chunk)
            acc_re = jnp.zeros((chunk, H), jnp.float32)
            acc_im = jnp.zeros((chunk, H), jnp.float32)
            for g in range(4):
                a_re = own[g : g + 1, :]
                a_im = own[4 + g : 5 + g, :]
                b_re = planes[g, cut, :]
                b_im = planes[4 + g, cut, :]
                acc_re = acc_re + a_re * b_re + a_im * b_im
                acc_im = acc_im + a_re * b_im - a_im * b_re
            place = pl.ds(pl.multiple_of(i * far_stations + start, chunk), chunk)
            cross[place, 0:H] = acc_re.astype(cross.dtype)
            cross[place, H:SEG] = acc_im.astype(cross.dtype)
        return carry

    lax.fori_loop(0, rows, one, 0)
    own_mask = own_mask_ref[0]
    far_mask = far_mask_ref[0]
    counts = far_mask[:, 0:1] * own_mask[0:1, :]
    for g in range(1, own_mask.shape[0]):
        counts = counts + far_mask[:, g : g + 1] * own_mask[g : g + 1, :]
    scale = 1.0 / (math.sqrt(SEG) * jnp.maximum(counts, 1.0))
    for first in range(0, rows * far_stations, band):
        summed = jnp.dot(
            cross[first : first + band, :], inverse_ref[...], preferred_element_type=jnp.float32
        )
        for piece in range(band // far_stations):
            i = first // far_stations + piece
            rows_of = summed[piece * far_stations : (piece + 1) * far_stations, :]
            out_ref[0, i] = (rows_of * scale[:, i : i + 1]).astype(out_ref.dtype)


def correlate(own_parts, far_planes, inverse, own_mask, far_masks, rows=16, chunk=32, band=256):
    stations = own_parts.shape[0]
    rounds, parts, far_stations, bins = far_planes.shape
    segments = own_mask.shape[1]
    own_mask = own_mask.astype(jnp.float32).reshape(stations // rows, rows, segments).transpose(0, 2, 1)
    return pl.pallas_call(
        functools.partial(correlate_kernel, rows=rows, chunk=chunk, band=band),
        grid=(rounds, stations // rows),
        in_specs=[
            pl.BlockSpec((rows, parts, bins), lambda r, b: (b, 0, 0)),
            pl.BlockSpec((1, parts, far_stations, bins), lambda r, b: (r, 0, 0, 0)),
            pl.BlockSpec((SEG, SEG), lambda r, b: (0, 0)),
            pl.BlockSpec((1, segments, rows), lambda r, b: (b, 0, 0)),
            pl.BlockSpec((1, far_stations, segments), lambda r, b: (r, 0, 0)),
        ],
        out_specs=pl.BlockSpec((1, rows, far_stations, SEG), lambda r, b: (r, b, 0, 0)),
        out_shape=jax.ShapeDtypeStruct((rounds, stations, far_stations, SEG), jnp.bfloat16),
        scratch_shapes=[
            pltpu.VMEM((parts, far_stations, bins), jnp.float32),
            pltpu.VMEM((rows * far_stations, SEG), jnp.bfloat16),
        ],
        compiler_params=pltpu.CompilerParams(dimension_semantics=("arbitrary", "arbitrary")),
    )(own_parts, far_planes, inverse, own_mask, far_masks.astype(jnp.float32))


def shards(records, record_station, taps, gap_mask, partners):
    per_block = taps.shape[0]
    block_total = lax.axis_size("dev")
    my_index = lax.axis_index("dev")
    ordered = place_records(records, record_station, per_block, block_total, my_index)
    own_spec = whiten(ordered, taps, gap_mask)
    mask_row = jnp.zeros((1, SEG), jnp.bfloat16).at[0, : per_block * NSEG].set(
        gap_mask.reshape(-1).astype(jnp.bfloat16)
    )
    payload = jnp.concatenate([own_spec.reshape(per_block * NSEG, SEG), mask_row], axis=0)
    rounds = partners.shape[0]
    codes = jnp.bitwise_xor(my_index, partners[:, my_index])

    gathered = jnp.stack(
        [exchange(payload, codes[round_index], block_total) for round_index in range(rounds)]
    )
    far = gathered[:, : per_block * NSEG].reshape(rounds, per_block, NSEG, SEG)
    far_masks = gathered[:, per_block * NSEG, : per_block * NSEG].reshape(rounds, per_block, NSEG)
    own_parts = jnp.concatenate([own_spec[..., :H], own_spec[..., H:]], axis=1)
    far_planes = jnp.concatenate([far[..., :H], far[..., H:]], axis=2).transpose(0, 2, 1, 3)
    return correlate(own_parts, far_planes, inverse_table(), gap_mask, far_masks)


def solution(mesh):
    in_specs = (P("dev", None), P("dev"), P("dev", None), P("dev", None), P())
    out_specs = P(None, "dev", None, None)
    return jax.shard_map(shards, mesh=mesh, in_specs=in_specs, out_specs=out_specs, check_vma=False)
```

```python
import functools
import math

import jax
import jax.numpy as jnp
from jax import lax
from jax.experimental import pallas as pl
from jax.experimental.pallas import tpu as pltpu
from jax.sharding import PartitionSpec as P

SEG = 512
H = SEG // 2
TAPS = 255
NSEG = 4


def angle_table(row_count, col_count):
    first = jnp.arange(row_count, dtype=jnp.int32)[:, None]
    second = jnp.arange(col_count, dtype=jnp.int32)[None, :]
    return 2.0 * math.pi / SEG * (first * second % SEG).astype(jnp.float32)


def forward_table(row_count):
    phase = angle_table(row_count, SEG // 2)
    return jnp.concatenate([jnp.cos(phase), -jnp.sin(phase)], axis=1).astype(jnp.bfloat16)


def inverse_table():
    phase = angle_table(SEG // 2, SEG)
    weights = jnp.where(jnp.arange(SEG // 2, dtype=jnp.int32) == 0, 1.0, 2.0).astype(jnp.float32)[
        :, None
    ]
    return jnp.concatenate([weights * jnp.cos(phase), -weights * jnp.sin(phase)], axis=0).astype(
        jnp.bfloat16
    )


def whiten(ordered, taps, gap_mask):
    station_count = ordered.shape[0]
    pieces = ordered.reshape(station_count, NSEG, SEG).astype(jnp.float32)
    scaled = pieces * lax.rsqrt(jnp.mean(pieces * pieces, axis=2, keepdims=True) + 1e-06)
    normed = scaled.astype(jnp.bfloat16)
    spectrum = jnp.dot(
        normed.reshape(station_count * NSEG, SEG),
        forward_table(SEG),
        preferred_element_type=jnp.float32,
    )
    spectrum = spectrum.reshape(station_count, NSEG, SEG)
    response = jnp.dot(taps, forward_table(TAPS), preferred_element_type=jnp.float32)[:, None, :]
    half_bins = SEG // 2
    spec_re = spectrum[:, :, :half_bins]
    spec_im = spectrum[:, :, half_bins:]
    resp_re = response[:, :, :half_bins]
    resp_im = response[:, :, half_bins:]
    weight = gap_mask.astype(jnp.float32)[:, :, None]
    white_re = (spec_re * resp_re - spec_im * resp_im) * weight
    white_im = (spec_re * resp_im + spec_im * resp_re) * weight
    return jnp.concatenate([white_re, white_im], axis=2).astype(jnp.bfloat16)


def place_records(records, record_station, per_block, block_total, my_index):
    owners = record_station // per_block
    label = (record_station - owners * per_block + 1).astype(records.dtype)
    tagged = jnp.concatenate(
        [records, jnp.broadcast_to(label[:, None], (records.shape[0], 128))], axis=1
    )
    slots = jnp.arange(block_total, dtype=jnp.int32)
    sending = (slots[:, None] == owners[None, :]).astype(records.dtype)
    outgoing = jnp.dot(sending, tagged, preferred_element_type=jnp.float32).astype(records.dtype)
    arrived = lax.all_to_all(outgoing, "dev", split_axis=0, concat_axis=0, tiled=True)
    local_rows = arrived[:, records.shape[1]].astype(jnp.int32) - 1
    places = jnp.arange(per_block, dtype=jnp.int32)
    taking = (places[:, None] == local_rows[None, :]).astype(records.dtype)
    return jnp.dot(
        taking, arrived[:, : records.shape[1]], preferred_element_type=jnp.float32
    ).astype(records.dtype)


def exchange(payload, code, device_total):
    levels = device_total.bit_length() - 1
    groups = [(0, min(3, levels))]
    if levels > 3:
        groups.append((3, levels - 3))

    def send(mask, value):
        pairs = [(source, source ^ mask) for source in range(device_total)]
        return lax.ppermute(value, "dev", pairs)

    for shift, width in groups:
        part = jnp.bitwise_and(jnp.right_shift(code, shift), 2**width - 1)
        branches = [lambda value: value] + [
            functools.partial(send, step << shift) for step in range(1, 2**width)
        ]
        payload = lax.switch(part, branches, payload)
    return payload


def correlate_kernel(
    own_ref, far_ref, inverse_ref, own_mask_ref, far_mask_ref, out_ref, planes, cross, *, rows, chunk, band
):
    far_stations = planes.shape[1]

    @pl.when(pl.program_id(1) == 0)
    def _():
        planes[...] = far_ref[0].astype(jnp.float32)

    def one(i, carry):
        own = own_ref[i].astype(jnp.float32)
        for start in range(0, far_stations, chunk):
            cut = pl.ds(start, chunk)
            acc_re = jnp.zeros((chunk, H), jnp.float32)
            acc_im = jnp.zeros((chunk, H), jnp.float32)
            for g in range(4):
                a_re = own[g : g + 1, :]
                a_im = own[4 + g : 5 + g, :]
                b_re = planes[g, cut, :]
                b_im = planes[4 + g, cut, :]
                acc_re = acc_re + a_re * b_re + a_im * b_im
                acc_im = acc_im + a_re * b_im - a_im * b_re
            place = pl.ds(pl.multiple_of(i * far_stations + start, chunk), chunk)
            cross[place, 0:H] = acc_re.astype(cross.dtype)
            cross[place, H:SEG] = acc_im.astype(cross.dtype)
        return carry

    lax.fori_loop(0, rows, one, 0)
    own_mask = own_mask_ref[0]
    far_mask = far_mask_ref[0]
    counts = far_mask[:, 0:1] * own_mask[0:1, :]
    for g in range(1, own_mask.shape[0]):
        counts = counts + far_mask[:, g : g + 1] * own_mask[g : g + 1, :]
    scale = 1.0 / (math.sqrt(SEG) * jnp.maximum(counts, 1.0))
    for first in range(0, rows * far_stations, band):
        summed = jnp.dot(
            cross[first : first + band, :], inverse_ref[...], preferred_element_type=jnp.float32
        )
        for piece in range(band // far_stations):
            i = first // far_stations + piece
            rows_of = summed[piece * far_stations : (piece + 1) * far_stations, :]
            out_ref[0, i] = (rows_of * scale[:, i : i + 1]).astype(out_ref.dtype)


def correlate(own_parts, far_planes, inverse, own_mask, far_masks, rows=16, chunk=32, band=256):
    stations = own_parts.shape[0]
    rounds, parts, far_stations, bins = far_planes.shape
    segments = own_mask.shape[1]
    own_mask = own_mask.astype(jnp.float32).reshape(stations // rows, rows, segments).transpose(0, 2, 1)
    return pl.pallas_call(
        functools.partial(correlate_kernel, rows=rows, chunk=chunk, band=band),
        grid=(rounds, stations // rows),
        in_specs=[
            pl.BlockSpec((rows, parts, bins), lambda r, b: (b, 0, 0)),
            pl.BlockSpec((1, parts, far_stations, bins), lambda r, b: (r, 0, 0, 0)),
            pl.BlockSpec((SEG, SEG), lambda r, b: (0, 0)),
            pl.BlockSpec((1, segments, rows), lambda r, b: (b, 0, 0)),
            pl.BlockSpec((1, far_stations, segments), lambda r, b: (r, 0, 0)),
        ],
        out_specs=pl.BlockSpec((1, rows, far_stations, SEG), lambda r, b: (r, b, 0, 0)),
        out_shape=jax.ShapeDtypeStruct((rounds, stations, far_stations, SEG), jnp.bfloat16),
        scratch_shapes=[
            pltpu.VMEM((parts, far_stations, bins), jnp.float32),
            pltpu.VMEM((rows * far_stations, SEG), jnp.bfloat16),
        ],
        compiler_params=pltpu.CompilerParams(dimension_semantics=("arbitrary", "arbitrary")),
    )(own_parts, far_planes, inverse, own_mask, far_masks.astype(jnp.float32))


def shards(records, record_station, taps, gap_mask, partners):
    per_block = taps.shape[0]
    block_total = lax.axis_size("dev")
    my_index = lax.axis_index("dev")
    ordered = place_records(records, record_station, per_block, block_total, my_index)
    own_spec = whiten(ordered, taps, gap_mask)
    mask_row = jnp.zeros((1, SEG), jnp.bfloat16).at[0, : per_block * NSEG].set(
        gap_mask.reshape(-1).astype(jnp.bfloat16)
    )
    payload = jnp.concatenate([own_spec.reshape(per_block * NSEG, SEG), mask_row], axis=0)
    rounds = partners.shape[0]
    codes = jnp.bitwise_xor(my_index, partners[:, my_index])

    arrived = [exchange(payload, codes[round_index], block_total) for round_index in range(rounds)]
    rows = per_block * NSEG
    far_planes = jnp.stack(
        [
            jnp.concatenate([joined[:rows, :H], joined[:rows, H:]], axis=0)
            .reshape(2, per_block, NSEG, H)
            .transpose(0, 2, 1, 3)
            .reshape(2 * NSEG, per_block, H)
            for joined in arrived
        ]
    )
    far_masks = jnp.stack([joined[rows, :rows].reshape(per_block, NSEG) for joined in arrived])
    own_parts = jnp.concatenate([own_spec[..., :H], own_spec[..., H:]], axis=1)
    return correlate(own_parts, far_planes, inverse_table(), gap_mask, far_masks)


def solution(mesh):
    in_specs = (P("dev", None), P("dev"), P("dev", None), P("dev", None), P())
    out_specs = P(None, "dev", None, None)
    return jax.shard_map(shards, mesh=mesh, in_specs=in_specs, out_specs=out_specs, check_vma=False)
```

```python
import functools
import math

import jax
import jax.numpy as jnp
from jax import lax
from jax.experimental import pallas as pl
from jax.experimental.pallas import tpu as pltpu
from jax.sharding import PartitionSpec as P

SEG = 512
H = SEG // 2
TAPS = 255
NSEG = 4


def angle_table(row_count, col_count):
    first = jnp.arange(row_count, dtype=jnp.int32)[:, None]
    second = jnp.arange(col_count, dtype=jnp.int32)[None, :]
    return 2.0 * math.pi / SEG * (first * second % SEG).astype(jnp.float32)


def forward_table(row_count):
    phase = angle_table(row_count, SEG // 2)
    return jnp.concatenate([jnp.cos(phase), -jnp.sin(phase)], axis=1).astype(jnp.bfloat16)


def inverse_table():
    phase = angle_table(SEG // 2, SEG)
    weights = jnp.where(jnp.arange(SEG // 2, dtype=jnp.int32) == 0, 1.0, 2.0).astype(jnp.float32)[
        :, None
    ]
    return jnp.concatenate([weights * jnp.cos(phase), -weights * jnp.sin(phase)], axis=0).astype(
        jnp.bfloat16
    )


def whiten(ordered, taps, gap_mask):
    station_count = ordered.shape[0]
    pieces = ordered.reshape(station_count, NSEG, SEG).astype(jnp.float32)
    scaled = pieces * lax.rsqrt(jnp.mean(pieces * pieces, axis=2, keepdims=True) + 1e-06)
    normed = scaled.astype(jnp.bfloat16)
    spectrum = jnp.dot(
        normed.reshape(station_count * NSEG, SEG),
        forward_table(SEG),
        preferred_element_type=jnp.float32,
    )
    spectrum = spectrum.reshape(station_count, NSEG, SEG)
    response = jnp.dot(taps, forward_table(TAPS), preferred_element_type=jnp.float32)[:, None, :]
    half_bins = SEG // 2
    spec_re = spectrum[:, :, :half_bins]
    spec_im = spectrum[:, :, half_bins:]
    resp_re = response[:, :, :half_bins]
    resp_im = response[:, :, half_bins:]
    weight = gap_mask.astype(jnp.float32)[:, :, None]
    white_re = (spec_re * resp_re - spec_im * resp_im) * weight
    white_im = (spec_re * resp_im + spec_im * resp_re) * weight
    return jnp.concatenate([white_re, white_im], axis=2).astype(jnp.bfloat16)


def place_records(records, record_station, per_block, block_total, my_index):
    owners = record_station // per_block
    label = (record_station - owners * per_block + 1).astype(records.dtype)
    tagged = jnp.concatenate(
        [records, jnp.broadcast_to(label[:, None], (records.shape[0], 128))], axis=1
    )
    slots = jnp.arange(block_total, dtype=jnp.int32)
    sending = (slots[:, None] == owners[None, :]).astype(records.dtype)
    outgoing = jnp.dot(sending, tagged, preferred_element_type=jnp.float32).astype(records.dtype)
    arrived = lax.all_to_all(outgoing, "dev", split_axis=0, concat_axis=0, tiled=True)
    local_rows = arrived[:, records.shape[1]].astype(jnp.int32) - 1
    places = jnp.arange(per_block, dtype=jnp.int32)
    taking = (places[:, None] == local_rows[None, :]).astype(records.dtype)
    return jnp.dot(
        taking, arrived[:, : records.shape[1]], preferred_element_type=jnp.float32
    ).astype(records.dtype)


def exchange(payload, code, device_total):
    levels = device_total.bit_length() - 1
    groups = [(0, min(3, levels))]
    if levels > 3:
        groups.append((3, levels - 3))

    def send(mask, value):
        pairs = [(source, source ^ mask) for source in range(device_total)]
        return lax.ppermute(value, "dev", pairs)

    for shift, width in groups:
        part = jnp.bitwise_and(jnp.right_shift(code, shift), 2**width - 1)
        branches = [lambda value: value] + [
            functools.partial(send, step << shift) for step in range(1, 2**width)
        ]
        payload = lax.switch(part, branches, payload)
    return payload


def correlate_kernel(
    own_ref, far_ref, inverse_ref, own_mask_ref, far_mask_ref, out_ref, planes, cross, *, rows, chunk, band
):
    far_stations = planes.shape[1]

    @pl.when(pl.program_id(1) == 0)
    def _():
        planes[...] = far_ref[0].astype(jnp.float32)

    def one(i, carry):
        own = own_ref[i].astype(jnp.float32)
        for start in range(0, far_stations, chunk):
            cut = pl.ds(start, chunk)
            acc_re = jnp.zeros((chunk, H), jnp.float32)
            acc_im = jnp.zeros((chunk, H), jnp.float32)
            for g in range(4):
                a_re = own[g : g + 1, :]
                a_im = own[4 + g : 5 + g, :]
                b_re = planes[g, cut, :]
                b_im = planes[4 + g, cut, :]
                acc_re = acc_re + a_re * b_re + a_im * b_im
                acc_im = acc_im + a_re * b_im - a_im * b_re
            place = pl.ds(pl.multiple_of(i * far_stations + start, chunk), chunk)
            cross[place, 0:H] = acc_re.astype(cross.dtype)
            cross[place, H:SEG] = acc_im.astype(cross.dtype)
        return carry

    lax.fori_loop(0, rows, one, 0)
    own_mask = own_mask_ref[0]
    far_mask = far_mask_ref[0]
    counts = far_mask[:, 0:1] * own_mask[0:1, :]
    for g in range(1, own_mask.shape[0]):
        counts = counts + far_mask[:, g : g + 1] * own_mask[g : g + 1, :]
    scale = 1.0 / (math.sqrt(SEG) * jnp.maximum(counts, 1.0))
    for first in range(0, rows * far_stations, band):
        summed = jnp.dot(
            cross[first : first + band, :], inverse_ref[...], preferred_element_type=jnp.float32
        )
        for piece in range(band // far_stations):
            i = first // far_stations + piece
            rows_of = summed[piece * far_stations : (piece + 1) * far_stations, :]
            out_ref[0, i] = (rows_of * scale[:, i : i + 1]).astype(out_ref.dtype)


def correlate(own_parts, far_planes, inverse, own_mask, far_masks, rows=32, chunk=32, band=256):
    stations = own_parts.shape[0]
    rounds, parts, far_stations, bins = far_planes.shape
    segments = own_mask.shape[1]
    own_mask = own_mask.astype(jnp.float32).reshape(stations // rows, rows, segments).transpose(0, 2, 1)
    return pl.pallas_call(
        functools.partial(correlate_kernel, rows=rows, chunk=chunk, band=band),
        grid=(rounds, stations // rows),
        in_specs=[
            pl.BlockSpec((rows, parts, bins), lambda r, b: (b, 0, 0)),
            pl.BlockSpec((1, parts, far_stations, bins), lambda r, b: (r, 0, 0, 0)),
            pl.BlockSpec((SEG, SEG), lambda r, b: (0, 0)),
            pl.BlockSpec((1, segments, rows), lambda r, b: (b, 0, 0)),
            pl.BlockSpec((1, far_stations, segments), lambda r, b: (r, 0, 0)),
        ],
        out_specs=pl.BlockSpec((1, rows, far_stations, SEG), lambda r, b: (r, b, 0, 0)),
        out_shape=jax.ShapeDtypeStruct((rounds, stations, far_stations, SEG), jnp.bfloat16),
        scratch_shapes=[
            pltpu.VMEM((parts, far_stations, bins), jnp.float32),
            pltpu.VMEM((rows * far_stations, SEG), jnp.bfloat16),
        ],
        compiler_params=pltpu.CompilerParams(dimension_semantics=("arbitrary", "arbitrary")),
    )(own_parts, far_planes, inverse, own_mask, far_masks.astype(jnp.float32))


def shards(records, record_station, taps, gap_mask, partners):
    per_block = taps.shape[0]
    block_total = lax.axis_size("dev")
    my_index = lax.axis_index("dev")
    ordered = place_records(records, record_station, per_block, block_total, my_index)
    own_spec = whiten(ordered, taps, gap_mask)
    mask_row = jnp.zeros((1, SEG), jnp.bfloat16).at[0, : per_block * NSEG].set(
        gap_mask.reshape(-1).astype(jnp.bfloat16)
    )
    payload = jnp.concatenate([own_spec.reshape(per_block * NSEG, SEG), mask_row], axis=0)
    rounds = partners.shape[0]
    codes = jnp.bitwise_xor(my_index, partners[:, my_index])

    gathered = jnp.stack(
        [exchange(payload, codes[round_index], block_total) for round_index in range(rounds)]
    )
    far = gathered[:, : per_block * NSEG].reshape(rounds, per_block, NSEG, SEG)
    far_masks = gathered[:, per_block * NSEG, : per_block * NSEG].reshape(rounds, per_block, NSEG)
    own_parts = jnp.concatenate([own_spec[..., :H], own_spec[..., H:]], axis=1)
    far_planes = jnp.concatenate([far[..., :H], far[..., H:]], axis=2).transpose(0, 2, 1, 3)
    return correlate(own_parts, far_planes, inverse_table(), gap_mask, far_masks)


def solution(mesh):
    in_specs = (P("dev", None), P("dev"), P("dev", None), P("dev", None), P())
    out_specs = P(None, "dev", None, None)
    return jax.shard_map(shards, mesh=mesh, in_specs=in_specs, out_specs=out_specs, check_vma=False)
```
